256 devices in a mesh: seq: 64 (over x, z, core), tensor: 4 (over y).
Axes of the slice: x: 4, y: 4, z: 8, core: 2. Of those that a mesh axis runs over, the one named last changes fastest.
Arguments:
- hidden: bfloat16 [8192, 8192], P('seq'), may hold values from -6 to 6
- gain: bfloat16 [8192], replicated, may hold values from 0.5 to 1.5
- w_query: bfloat16 [8192, 4096], P('seq', 'tensor'), may hold values from -0.0625 to 0.0625
- q_bias: bfloat16 [4096], P('tensor'), may hold values from -3 to 3
- w_keyval: bfloat16 [8192, 2, 512], P('seq', None, 'tensor'), may hold values from -0.125 to 0.125
- kv_bias: bfloat16 [2, 512], P(None, 'tensor'), may hold values from -3 to 3
- prefix_keys: bfloat16 [2, 4096, 4, 128], P(None, 'seq', 'tensor'), may hold values from -128 to 128, as said below
- prefix_values: bfloat16 [2, 4096, 4, 128], P(None, 'seq', 'tensor'), may hold values from -6 to 6
- lengths: int32 [32], replicated, may hold values from 1 to 384, 8192 in all
- assignment: int32 [32], replicated, may hold values from 0 to 1
Outputs:
- attention: bfloat16 [8192, 4096], P('seq', 'tensor')
- suffix_keys: bfloat16 [8192, 4, 128], P('seq', 'tensor')
- suffix_values: bfloat16 [8192, 4, 128], P('seq', 'tensor')
The draws below stay inside these ranges and needn't reach their ends.
Inputs may be any that keep to these rules, and one draw needn't show every extreme that they name: Request r occupies the next lengths[r] rows of the token arrays, in order; the lengths sum to 8192 and the largest is 384. `assignment`: the prefix that request r continues. `prefix_keys`: cached keys, already rotated to positions 0 to 4095.
All inputs are finite; a program needn't handle non-finite values.
Results may differ from the reference program's by a relative error of at most 0.01.
The reference program's roundings to bfloat16 on the way count: a program that leaves them out, or rounds other values in their place, can miss the bound.
Values may be sent and summed in bfloat16 or wider, within the bound.
No kernel may reach another device: no remote copies, remote signals or barrier semaphores. Data moves between devices by JAX's collectives and lax.ppermute only.
A program may use at most 128 MiB of HBM per device.

```python
import math
import jax
import jax.numpy as jnp
import numpy as np
from jax import lax

D = 8192
HEADS = 32
KV_HEADS = 4
HEAD_DIM = 128
GROUP = 8
TOKENS = 8192
REQUESTS = 32
PREFIXES = 2
PLEN = 4096
MAXLEN = 384


def draw_prefix_keys(key, part):
    base_key = jax.random.fold_in(key, 0)
    shape = (PREFIXES, PLEN // 2, 2, KV_HEADS, HEAD_DIM)
    drawn = jnp.clip(jax.random.normal(base_key, shape, jnp.float32), -6.0, 6.0)
    return drawn.reshape(PREFIXES, PLEN, KV_HEADS, HEAD_DIM).astype(jnp.bfloat16)


def place_ends(entries, own_key, low, largest):
    longest = entries.shape.index(max(entries.shape))
    spots = []
    for shift in (0, 1):
        where = [jax.random.randint(jax.random.fold_in(own_key, axis), (), 0, length) for axis, length in enumerate(entries.shape)]
        where[longest] = (where[longest] + shift) % entries.shape[longest]
        spots.append(tuple(where))
    return entries.at[spots[0]].set(low).at[spots[1]].set(largest)


def levels(key, dims, cuts, smallest, largest):
    level = 1.0
    for position, shards_of in cuts:
        heights = jax.random.uniform(jax.random.fold_in(jax.random.fold_in(key, 6), position), (shards_of,), jnp.float32, smallest / len(cuts), largest / len(cuts))
        level = level * jnp.repeat(jnp.exp(heights), dims[position] // shards_of).reshape((-1,) + (1,) * (len(dims) - 1 - position))
    return level


def profile(count, total, most, slope):
    loads = [(1 << 20) // math.isqrt(rank ** slope) + 1 for rank in range(2, count + 1)]
    spare, holding = total - most - (count - 1), [1] * (count - 1)
    while spare > 0:
        candidates = [i for i in range(count - 1) if holding[i] < most]
        whole, remaining = sum([loads[i] for i in candidates]), spare
        for i in candidates:
            extra = min(most - holding[i], max(1, remaining * loads[i] // whole), spare)
            holding[i] = holding[i] + extra
            spare = spare - extra
    return np.array([most] + holding)


def uneven(stream_key, number_of, total, bound, slope):
    if number_of == 2:
        one = jax.random.randint(stream_key, (), max(1, total - bound), min(bound, total - 1) + 1)
        return jnp.stack([one, total - one])
    sizes = jnp.asarray(profile(number_of, total, bound, slope), jnp.int32)
    couples = (number_of - 1) // 2
    donor, sink = sizes[1:1 + 2 * couples:2], sizes[2:2 + 2 * couples:2]
    margin = jnp.minimum(donor - 1, bound - sink)
    moved = jax.random.randint(jax.random.fold_in(stream_key, 1), (couples,), 0, 1 << 20) % (margin + 1)
    sizes = sizes.at[1:1 + 2 * couples:2].set(donor - moved).at[2:2 + 2 * couples:2].set(sink + moved)
    return sizes[jax.random.permutation(jax.random.fold_in(stream_key, 2), number_of)]


def normal_values(key, extent, scale, bound, cuts=(), kind=jnp.bfloat16):
    level = levels(key, extent, cuts, -0.22, 0.18) if cuts else 1.0
    entries = jax.random.normal(key, extent, jnp.float32) * scale * level
    return jnp.minimum(jnp.maximum(entries, -bound), bound).astype(kind)


def setup_inputs(seed: int = 0) -> dict:
    keys = jax.random.split(jax.random.key(seed), 11)
    hidden = normal_values(keys[0], (TOKENS, D), 1.0, 6.0, ((0, 64),))
    gain = jnp.clip(1.0 + 0.1 * jax.random.normal(keys[1], (D,), jnp.float32), 0.5, 1.5).astype(jnp.bfloat16)
    w_query = normal_values(keys[2], (D, HEADS * HEAD_DIM), D ** -0.5, 0.0625, ((0, 64), (1, 4)))
    q_bias = normal_values(keys[3], (HEADS * HEAD_DIM,), 0.5, 3.0, ((0, 4),))
    w_keyval = normal_values(keys[4], (D, 2, KV_HEADS * HEAD_DIM), (D // 4) ** -0.5, 0.125, ((0, 64), (2, 4)))
    kv_bias = normal_values(keys[5], (2, KV_HEADS * HEAD_DIM), 0.5, 3.0, ((1, 4),))
    prefix_keys = draw_prefix_keys(jax.random.fold_in(keys[10], 71), 0)
    prefix_values = normal_values(keys[7], (PREFIXES, PLEN, KV_HEADS, HEAD_DIM), 1.0, 6.0, ((1, 64), (2, 4)))
    lengths = uneven(keys[8], REQUESTS, TOKENS, MAXLEN, 1).astype(jnp.int32)
    assignment = place_ends(jax.random.randint(keys[9], (REQUESTS,), 0, PREFIXES), jax.random.fold_in(keys[9], 1), 0, PREFIXES - 1).astype(jnp.int32)
    return dict(hidden=hidden, gain=gain, w_query=w_query, q_bias=q_bias, w_keyval=w_keyval, kv_bias=kv_bias, prefix_keys=prefix_keys, prefix_values=prefix_values, lengths=lengths, assignment=assignment)


EPS = 1e-06
THETA = 1000000.0

def row_tables(lengths, assignment, all_rows):
    request_end = jnp.cumsum(lengths).astype(jnp.int32)
    request_start = (request_end - lengths).astype(jnp.int32)
    row_ids = jnp.arange(all_rows, dtype=jnp.int32)
    segment = lax.optimization_barrier(jnp.sum((row_ids[:, None] >= request_end[None, :]).astype(jnp.int32), axis=1)).astype(jnp.int32)
    request_ids = jnp.arange(lengths.shape[0], dtype=jnp.int32)
    onehot = (segment[:, None] == request_ids[None, :]).astype(jnp.int32)
    offset = (row_ids - lax.optimization_barrier(jnp.sum(onehot * request_start[None, :], axis=1))).astype(jnp.int32)
    prefix = lax.optimization_barrier(jnp.sum(onehot * assignment[None, :], axis=1)).astype(jnp.int32)
    return (segment, offset, prefix)

def rotate(values, positions):
    head_size = values.shape[-1]
    half_dim = head_size // 2
    frequency = THETA ** (-2.0 * jnp.arange(half_dim, dtype=jnp.float32) / head_size)
    angles = positions.astype(jnp.float32)[:, None] * frequency[None, :]
    cosine = jnp.concatenate([jnp.cos(angles), jnp.cos(angles)], axis=-1)[:, None, :]
    sine_part = jnp.concatenate([jnp.sin(angles), jnp.sin(angles)], axis=-1)[:, None, :]
    turned = jnp.concatenate([-values[..., half_dim:], values[..., :half_dim]], axis=-1)
    return values * cosine + turned * sine_part

def reference(hidden, gain, w_query, q_bias, w_keyval, kv_bias, prefix_keys, prefix_values, lengths, assignment):
    all_rows = hidden.shape[0]
    hidden_f = hidden.astype(jnp.float32)
    normed = (hidden_f * lax.rsqrt(lax.optimization_barrier(jnp.mean(hidden_f * hidden_f, axis=1, keepdims=True)) + EPS) * gain.astype(jnp.float32)).astype(jnp.bfloat16)
    query = jnp.dot(normed, w_query, preferred_element_type=jnp.float32) + q_bias.astype(jnp.float32)
    pair_width = 2 * KV_HEADS * HEAD_DIM
    key_width = KV_HEADS * HEAD_DIM
    pairs = jnp.dot(normed, w_keyval.reshape(D, pair_width), preferred_element_type=jnp.float32) + kv_bias.reshape(pair_width).astype(jnp.float32)
    segment, offset, prefix = row_tables(lengths, assignment, all_rows)
    positions = (offset + PLEN).astype(jnp.int32)
    queries = rotate(query.reshape(all_rows, HEADS, HEAD_DIM), positions).astype(jnp.bfloat16)
    suffix_keys = rotate(pairs[:, :key_width].reshape(all_rows, KV_HEADS, HEAD_DIM), positions).astype(jnp.bfloat16)
    suffix_values = pairs[:, key_width:].reshape(all_rows, KV_HEADS, HEAD_DIM).astype(jnp.bfloat16)
    block_rows = math.gcd(all_rows, 32)
    block_count = all_rows // block_rows
    row_ids = jnp.arange(all_rows, dtype=jnp.int32)
    score_scale = HEAD_DIM ** (-0.5)
    cache_keys = prefix_keys.astype(jnp.float32)
    cache_values = prefix_values.astype(jnp.float32)
    near_keys = suffix_keys.astype(jnp.float32)
    near_values = suffix_values.astype(jnp.float32)
    prefix_ids = jnp.arange(PREFIXES, dtype=jnp.int32)

    def attend(pieces):
        query_block, owner, seg_block, row_block = pieces
        query_f = query_block.astype(jnp.float32).reshape(block_rows, KV_HEADS, GROUP, HEAD_DIM)
        far_scores = jnp.einsum('bgqd,plgd->bgqpl', query_f, cache_keys) * score_scale
        allowed = (owner[:, None] == prefix_ids[None, :])[:, None, None, :, None]
        far_scores = jnp.where(allowed, far_scores, -jnp.inf)
        near_scores = jnp.einsum('bgqd,ngd->bgqn', query_f, near_keys) * score_scale
        visible = (segment[None, :] == seg_block[:, None]) & (row_ids[None, :] <= row_block[:, None])
        near_scores = jnp.where(visible[:, None, None, :], near_scores, -jnp.inf)
        row_top = jnp.maximum(lax.optimization_barrier(jnp.max(far_scores, axis=(3, 4))), lax.optimization_barrier(jnp.max(near_scores, axis=3)))
        far_weights = jnp.exp(far_scores - row_top[..., None, None])
        near_weights = jnp.exp(near_scores - row_top[..., None])
        row_mass = lax.optimization_barrier(jnp.sum(far_weights, axis=(3, 4))) + lax.optimization_barrier(jnp.sum(near_weights, axis=3))
        far_round = far_weights.astype(jnp.bfloat16).astype(jnp.float32)
        near_round = near_weights.astype(jnp.bfloat16).astype(jnp.float32)
        row_acc = jnp.einsum('bgqpl,plgd->bgqd', far_round, cache_values) + jnp.einsum('bgqn,ngd->bgqd', near_round, near_values)
        return (row_acc / row_mass[..., None]).astype(jnp.bfloat16)
    blocks = lax.map(attend, (queries.reshape(block_count, block_rows, HEADS, HEAD_DIM), prefix.reshape(block_count, block_rows), segment.reshape(block_count, block_rows), row_ids.reshape(block_count, block_rows)))
    attention = blocks.reshape(all_rows, HEADS * HEAD_DIM)
    return (attention, suffix_keys, suffix_values)
```

```python
import math

import jax
import jax.numpy as jnp
from jax import lax
from jax.experimental import pallas as pl
from jax.experimental.pallas import tpu as pltpu
from jax.sharding import Mesh
from jax.sharding import PartitionSpec as P

EPS = 1e-06
THETA = 1000000.0
SEQ = ("sx", "sc")


def from_behind(shard, axis, by):
    size = lax.axis_size(axis)
    pairs = [(i, i + by) for i in range(size) if 0 <= i + by < size]
    return lax.ppermute(shard, axis, pairs)


def row_tables(lengths, assignment, all_rows):
    request_end = jnp.cumsum(lengths)
    request_start = request_end - lengths
    row_ids = jnp.arange(all_rows, dtype=jnp.int32)
    segment = jnp.sum((row_ids[:, None] >= request_end[None, :]).astype(jnp.int32), axis=1)
    request_ids = jnp.arange(lengths.shape[0], dtype=jnp.int32)
    onehot = (segment[:, None] == request_ids[None, :]).astype(jnp.int32)
    offset = row_ids - jnp.sum(onehot * request_start[None, :], axis=1)
    prefix = jnp.sum(onehot * assignment[None, :], axis=1)
    return (segment, offset, prefix)


def rotate(values, positions):
    head_size = values.shape[-1]
    half_dim = head_size // 2
    frequency = THETA ** (-2.0 * jnp.arange(half_dim, dtype=jnp.float32) / head_size)
    angles = positions.astype(jnp.float32)[:, None] * frequency[None, :]
    cosine = jnp.concatenate([jnp.cos(angles), jnp.cos(angles)], axis=-1)[:, None, :]
    sine_part = jnp.concatenate([jnp.sin(angles), jnp.sin(angles)], axis=-1)[:, None, :]
    turned = jnp.concatenate([-values[..., half_dim:], values[..., :half_dim]], axis=-1)
    return values * cosine + turned * sine_part


def attention_kernel(q_ref, row_ref, col_ref, kv_ref, near_ref, o_ref, *, head_dim, scale):
    d = head_dim
    dims = (((1,), (1,)), ((), ()))
    q = q_ref[...]
    rows = row_ref[...]
    use_first = rows[:, 0:1] == 0
    row_seg = rows[:, 1:2]
    row_idx = rows[:, 2:3]
    cols = col_ref[...]
    far0 = lax.dot_general(q, kv_ref[:, 0:d], dims, preferred_element_type=jnp.float32) * scale
    far1 = lax.dot_general(q, kv_ref[:, d : 2 * d], dims, preferred_element_type=jnp.float32) * scale
    far = jnp.where(use_first, far0, far1)
    near = lax.dot_general(q, near_ref[:, 0:d], dims, preferred_element_type=jnp.float32) * scale
    visible = (cols[0:1, :] == row_seg) & (cols[1:2, :] <= row_idx)
    near = jnp.where(visible, near, -jnp.inf)
    top = jnp.maximum(jnp.max(far, axis=1, keepdims=True), jnp.max(near, axis=1, keepdims=True))
    far_w = jnp.exp(far - top)
    near_w = jnp.exp(near - top)
    mass = jnp.sum(far_w, axis=1, keepdims=True) + jnp.sum(near_w, axis=1, keepdims=True)
    far_b = far_w.astype(jnp.bfloat16)
    zero = jnp.zeros_like(far_b)
    acc = jnp.dot(jnp.where(use_first, far_b, zero), kv_ref[:, 2 * d : 3 * d], preferred_element_type=jnp.float32)
    acc = acc + jnp.dot(jnp.where(use_first, zero, far_b), kv_ref[:, 3 * d : 4 * d], preferred_element_type=jnp.float32)
    acc = acc + jnp.dot(near_w.astype(jnp.bfloat16), near_ref[:, d : 2 * d], preferred_element_type=jnp.float32)
    o_ref[...] = (acc / mass).astype(o_ref.dtype)


def attend(q_rows, row_info, col_info, kv_slab, near_slab, head_dim):
    n_rows = q_rows.shape[0]
    block = math.gcd(n_rows, 256)
    cache_len = kv_slab.shape[0]
    near_len = near_slab.shape[0]
    kernel = lambda *refs: attention_kernel(*refs, head_dim=head_dim, scale=head_dim ** (-0.5))
    keys_total = 2 * cache_len + near_len
    cost = pl.CostEstimate(
        flops=4 * n_rows * keys_total * head_dim,
        transcendentals=n_rows * (cache_len + near_len),
        bytes_accessed=kv_slab.size * 2 + near_slab.size * 2 + q_rows.size * 4,
    )
    return pl.pallas_call(
        kernel,
        grid=(n_rows // block,),
        in_specs=[
            pl.BlockSpec((block, head_dim), lambda i: (i, 0)),
            pl.BlockSpec((block, row_info.shape[1]), lambda i: (i, 0)),
            pl.BlockSpec(col_info.shape, lambda i: (0, 0)),
            pl.BlockSpec(kv_slab.shape, lambda i: (0, 0)),
            pl.BlockSpec(near_slab.shape, lambda i: (0, 0)),
        ],
        out_specs=pl.BlockSpec((block, head_dim), lambda i: (i, 0)),
        out_shape=jax.ShapeDtypeStruct((n_rows, head_dim), jnp.bfloat16),
        cost_estimate=cost,
        compiler_params=pltpu.CompilerParams(vmem_limit_bytes=48 * 1024 * 1024),
    )(q_rows, row_info, col_info, kv_slab, near_slab)


def local(
    hidden,
    gain,
    w_query,
    q_bias,
    w_keyval,
    kv_bias,
    prefix_keys,
    prefix_values,
    lengths,
    assignment,
):
    row_count = hidden.shape[0]
    pair_count = lax.axis_size("sc")
    seq_count = lax.axis_size("sx") * pair_count
    seq_index = lax.axis_index("sx") * pair_count + lax.axis_index("sc")
    all_rows = row_count * seq_count
    head_dim = prefix_keys.shape[3]
    kv_local = prefix_keys.shape[2]
    query_width = w_query.shape[1]
    heads_local = query_width // head_dim
    pair_width = w_keyval.shape[1] * w_keyval.shape[2]
    key_width = pair_width // 2
    cache_length = prefix_keys.shape[1] * seq_count
    first_row = seq_index * row_count
    hidden_f = hidden.astype(jnp.float32)
    normed = (
        hidden_f
        * lax.rsqrt(jnp.mean(hidden_f * hidden_f, axis=1, keepdims=True) + EPS)
        * gain.astype(jnp.float32)
    ).astype(jnp.bfloat16)
    segment, offset, prefix = row_tables(lengths, assignment, all_rows)
    positions = offset + cache_length
    own_positions = lax.dynamic_slice_in_dim(positions, first_row, row_count)
    own_segment = lax.dynamic_slice_in_dim(segment, first_row, row_count)
    own_prefix = lax.dynamic_slice_in_dim(prefix, first_row, row_count)

    slab = jnp.concatenate(
        [prefix_keys[0, :, 0, :], prefix_keys[1, :, 0, :], prefix_values[0, :, 0, :], prefix_values[1, :, 0, :]],
        axis=1,
    )

    w_pairs = w_keyval.reshape(w_keyval.shape[0], pair_width)
    combined = jnp.concatenate([w_query, w_pairs], axis=1)
    total_width = combined.shape[1]
    half_width = total_width // pair_count
    halves = lax.all_to_all(
        combined.reshape(row_count, pair_count, half_width), "sc", 1, 0, tiled=True
    ).reshape(row_count * pair_count, half_width)
    w_half = lax.all_gather(halves, "sx", axis=0, tiled=True)
    kv_slab = lax.all_gather(slab, SEQ, axis=0, tiled=True)
    normed_pair = lax.all_gather(normed, "sc", axis=0, tiled=True)
    part = jnp.dot(normed_pair, w_half, preferred_element_type=jnp.float32)
    summed = lax.all_to_all(
        part.reshape(pair_count, row_count, 1, half_width), "sc", 0, 2, tiled=True
    ).reshape(row_count, total_width)
    bias = jnp.concatenate([q_bias, kv_bias.reshape(pair_width)]).astype(jnp.float32)
    summed = summed + bias
    query_own = summed[:, :query_width]
    pairs_own = summed[:, query_width:]
    own_queries = rotate(query_own.reshape(row_count, heads_local, head_dim), own_positions).astype(
        jnp.bfloat16
    )
    own_keys = rotate(
        pairs_own[:, :key_width].reshape(row_count, kv_local, head_dim), own_positions
    ).astype(jnp.bfloat16)
    own_values = (
        pairs_own[:, key_width:].reshape(row_count, kv_local, head_dim).astype(jnp.bfloat16)
    )
    pair_rows = jnp.concatenate(
        [own_keys.reshape(row_count, key_width), own_values.reshape(row_count, key_width)], axis=1
    )
    depth = min(3, seq_count - 1)
    earlier = []
    for distance in range(depth, 0, -1):
        earlier.append(from_behind(pair_rows, SEQ, distance))
    near_rows = jnp.concatenate(earlier + [pair_rows], axis=0)
    near_count = near_rows.shape[0]
    near_index = first_row - depth * row_count + jnp.arange(near_count, dtype=jnp.int32)
    near_segment = segment[jnp.clip(near_index, 0, all_rows - 1)]
    near_segment = jnp.where(near_index >= 0, near_segment, -1)
    col_info = jnp.concatenate(
        [near_segment[None, :], near_index[None, :], jnp.zeros((6, near_count), jnp.int32)], axis=0
    )
    own_rows = first_row + jnp.arange(row_count, dtype=jnp.int32)
    row_info = jnp.stack(
        [own_prefix, own_segment, own_rows, jnp.zeros_like(own_rows)], axis=1
    ).astype(jnp.int32)
    row_info = jnp.repeat(row_info, heads_local, axis=0)
    out_rows = attend(
        own_queries.reshape(row_count * heads_local, head_dim),
        row_info,
        col_info,
        kv_slab,
        near_rows,
        head_dim,
    )
    attention = out_rows.reshape(row_count, query_width)
    return (attention, own_keys, own_values)


def solution(mesh):
    seq_size = mesh.shape["seq"]
    grid = Mesh(
        mesh.devices.reshape(seq_size // 2, 2, mesh.shape["tensor"]), ("sx", "sc", "tensor")
    )
    in_specs = (
        P(SEQ, None),
        P(),
        P(SEQ, "tensor"),
        P("tensor"),
        P(SEQ, None, "tensor"),
        P(None, "tensor"),
        P(None, SEQ, "tensor", None),
        P(None, SEQ, "tensor", None),
        P(),
        P(),
    )
    out_specs = (P(SEQ, "tensor"), P(SEQ, "tensor", None), P(SEQ, "tensor", None))
    return jax.shard_map(local, mesh=grid, in_specs=in_specs, out_specs=out_specs, check_vma=False)
```

```python
import math

import jax
import jax.numpy as jnp
from jax import lax
from jax.experimental import pallas as pl
from jax.experimental.pallas import tpu as pltpu
from jax.sharding import PartitionSpec as P

EPS = 1e-06
THETA = 1000000.0


def from_behind(shard, axis, by):
    size = lax.axis_size(axis)
    pairs = [(i, i + by) for i in range(size) if 0 <= i + by < size]
    return lax.ppermute(shard, axis, pairs)


def row_tables(lengths, assignment, all_rows):
    request_end = jnp.cumsum(lengths)
    request_start = request_end - lengths
    row_ids = jnp.arange(all_rows, dtype=jnp.int32)
    segment = jnp.sum((row_ids[:, None] >= request_end[None, :]).astype(jnp.int32), axis=1)
    request_ids = jnp.arange(lengths.shape[0], dtype=jnp.int32)
    onehot = (segment[:, None] == request_ids[None, :]).astype(jnp.int32)
    offset = row_ids - jnp.sum(onehot * request_start[None, :], axis=1)
    prefix = jnp.sum(onehot * assignment[None, :], axis=1)
    return (segment, offset, prefix)


def rotate(values, positions):
    head_size = values.shape[-1]
    half_dim = head_size // 2
    frequency = THETA ** (-2.0 * jnp.arange(half_dim, dtype=jnp.float32) / head_size)
    angles = positions.astype(jnp.float32)[:, None] * frequency[None, :]
    cosine = jnp.concatenate([jnp.cos(angles), jnp.cos(angles)], axis=-1)[:, None, :]
    sine_part = jnp.concatenate([jnp.sin(angles), jnp.sin(angles)], axis=-1)[:, None, :]
    turned = jnp.concatenate([-values[..., half_dim:], values[..., :half_dim]], axis=-1)
    return values * cosine + turned * sine_part


def attention_kernel(q_ref, row_ref, col_ref, kv_ref, near_ref, o_ref, *, head_dim, packs, scale):
    d = head_dim
    dims = (((1,), (1,)), ((), ()))
    q = q_ref[...]
    rows = row_ref[...]
    use_first = rows[:, 0:1] == 0
    row_seg = rows[:, 1:2]
    row_idx = rows[:, 2:3]
    cols = col_ref[...]
    n_dev, n_sub = kv_ref.shape[0], kv_ref.shape[1]

    def piece(j):
        return kv_ref[:, :, j * d : (j + 1) * d].reshape(n_dev * n_sub, d)

    far = []
    for k in range(packs):
        far0 = lax.dot_general(q, piece(4 * k), dims, preferred_element_type=jnp.float32) * scale
        far1 = lax.dot_general(q, piece(4 * k + 1), dims, preferred_element_type=jnp.float32) * scale
        far.append(jnp.where(use_first, far0, far1))
    near = lax.dot_general(q, near_ref[:, 0:d], dims, preferred_element_type=jnp.float32) * scale
    visible = (cols[0:1, :] == row_seg) & (cols[1:2, :] <= row_idx)
    near = jnp.where(visible, near, -jnp.inf)
    top = jnp.max(near, axis=1, keepdims=True)
    for s in far:
        top = jnp.maximum(top, jnp.max(s, axis=1, keepdims=True))
    near_w = jnp.exp(near - top)
    mass = jnp.sum(near_w, axis=1, keepdims=True)
    acc = jnp.dot(near_w.astype(jnp.bfloat16), near_ref[:, d : 2 * d], preferred_element_type=jnp.float32)
    for k, s in enumerate(far):
        far_w = jnp.exp(s - top)
        mass = mass + jnp.sum(far_w, axis=1, keepdims=True)
        far_b = far_w.astype(jnp.bfloat16)
        zero = jnp.zeros_like(far_b)
        acc = acc + jnp.dot(jnp.where(use_first, far_b, zero), piece(4 * k + 2), preferred_element_type=jnp.float32)
        acc = acc + jnp.dot(jnp.where(use_first, zero, far_b), piece(4 * k + 3), preferred_element_type=jnp.float32)
    o_ref[...] = (acc / mass).astype(o_ref.dtype)


def attend(q_rows, row_info, col_info, gathered, kv_block, kv_rows, near_slab, head_dim):
    n_rows = q_rows.shape[0]
    block = math.gcd(n_rows, 256)
    n_dev = gathered.shape[0]
    width = gathered.shape[2]
    packs = width // (4 * head_dim)
    cache_len = n_dev * kv_rows * packs
    near_len = near_slab.shape[0]
    kernel = lambda *refs: attention_kernel(*refs, head_dim=head_dim, packs=packs, scale=head_dim ** (-0.5))
    keys_total = 2 * cache_len + near_len
    cost = pl.CostEstimate(
        flops=4 * n_rows * keys_total * head_dim,
        transcendentals=n_rows * (cache_len + near_len),
        bytes_accessed=n_dev * kv_rows * width * 2 + near_slab.size * 2 + q_rows.size * 4,
    )
    return pl.pallas_call(
        kernel,
        grid=(n_rows // block,),
        in_specs=[
            pl.BlockSpec((block, head_dim), lambda i: (i, 0)),
            pl.BlockSpec((block, row_info.shape[1]), lambda i: (i, 0)),
            pl.BlockSpec(col_info.shape, lambda i: (0, 0)),
            pl.BlockSpec((n_dev, kv_rows, width), lambda i: (0, kv_block, 0)),
            pl.BlockSpec(near_slab.shape, lambda i: (0, 0)),
        ],
        out_specs=pl.BlockSpec((block, head_dim), lambda i: (i, 0)),
        out_shape=jax.ShapeDtypeStruct((n_rows, head_dim), jnp.bfloat16),
        cost_estimate=cost,
        compiler_params=pltpu.CompilerParams(vmem_limit_bytes=48 * 1024 * 1024),
    )(q_rows, row_info, col_info, gathered, near_slab)


def local(
    hidden,
    gain,
    w_query,
    q_bias,
    w_keyval,
    kv_bias,
    prefix_keys,
    prefix_values,
    lengths,
    assignment,
):
    row_count = hidden.shape[0]
    seq_count = lax.axis_size("seq")
    seq_index = lax.axis_index("seq")
    all_rows = row_count * seq_count
    head_dim = prefix_keys.shape[3]
    kv_local = prefix_keys.shape[2]
    query_width = w_query.shape[1]
    heads_local = query_width // head_dim
    pair_width = w_keyval.shape[1] * w_keyval.shape[2]
    key_width = pair_width // 2
    cache_local = prefix_keys.shape[1]
    cache_length = cache_local * seq_count
    first_row = seq_index * row_count
    hidden_f = hidden.astype(jnp.float32)
    normed = (
        hidden_f
        * lax.rsqrt(jnp.mean(hidden_f * hidden_f, axis=1, keepdims=True) + EPS)
        * gain.astype(jnp.float32)
    ).astype(jnp.bfloat16)
    segment, offset, prefix = row_tables(lengths, assignment, all_rows)
    positions = offset + cache_length
    own_positions = lax.dynamic_slice_in_dim(positions, first_row, row_count)
    own_segment = lax.dynamic_slice_in_dim(segment, first_row, row_count)
    own_prefix = lax.dynamic_slice_in_dim(prefix, first_row, row_count)

    w_pairs = w_keyval.reshape(w_keyval.shape[0], pair_width)
    combined = jnp.concatenate([w_query, w_pairs], axis=1)
    total_width = combined.shape[1]
    entry = 4 * head_dim
    packs = total_width // entry
    kv_rows = -(-cache_local // packs)
    kv_rows = -(-kv_rows // 16) * 16
    slab = jnp.concatenate(
        [prefix_keys[0, :, 0, :], prefix_keys[1, :, 0, :], prefix_values[0, :, 0, :], prefix_values[1, :, 0, :]],
        axis=1,
    )
    slab = jnp.pad(slab, ((0, kv_rows * packs - cache_local), (0, 0)))
    slab = slab.reshape(packs, kv_rows, entry).transpose(1, 0, 2).reshape(kv_rows, packs * entry)
    slab = jnp.pad(slab, ((0, 0), (0, total_width - packs * entry)))
    assert kv_rows * packs == cache_local and row_count % kv_rows == 0
    block_rows = row_count + kv_rows
    gathered = lax.all_gather(jnp.concatenate([combined, slab], axis=0), "seq", axis=0, tiled=True)
    gathered = gathered.reshape(seq_count, block_rows, total_width)
    w_full = gathered[:, :row_count, :].reshape(seq_count * row_count, total_width)
    summed = jnp.dot(normed, w_full, preferred_element_type=jnp.float32)
    bias = jnp.concatenate([q_bias, kv_bias.reshape(pair_width)]).astype(jnp.float32)
    summed = summed + bias
    query_own = summed[:, :query_width]
    pairs_own = summed[:, query_width:]
    own_queries = rotate(query_own.reshape(row_count, heads_local, head_dim), own_positions).astype(
        jnp.bfloat16
    )
    own_keys = rotate(
        pairs_own[:, :key_width].reshape(row_count, kv_local, head_dim), own_positions
    ).astype(jnp.bfloat16)
    own_values = (
        pairs_own[:, key_width:].reshape(row_count, kv_local, head_dim).astype(jnp.bfloat16)
    )
    pair_rows = jnp.concatenate(
        [own_keys.reshape(row_count, key_width), own_values.reshape(row_count, key_width)], axis=1
    )
    depth = min(3, seq_count - 1)
    earlier = []
    for distance in range(depth, 0, -1):
        earlier.append(from_behind(pair_rows, "seq", distance))
    near_rows = jnp.concatenate(earlier + [pair_rows], axis=0)
    near_count = near_rows.shape[0]
    near_index = first_row - depth * row_count + jnp.arange(near_count, dtype=jnp.int32)
    near_segment = segment[jnp.clip(near_index, 0, all_rows - 1)]
    near_segment = jnp.where(near_index >= 0, near_segment, -1)
    col_info = jnp.concatenate(
        [near_segment[None, :], near_index[None, :], jnp.zeros((6, near_count), jnp.int32)], axis=0
    )
    own_rows = first_row + jnp.arange(row_count, dtype=jnp.int32)
    row_info = jnp.stack(
        [own_prefix, own_segment, own_rows, jnp.zeros_like(own_rows)], axis=1
    ).astype(jnp.int32)
    row_info = jnp.repeat(row_info, heads_local, axis=0)
    out_rows = attend(
        own_queries.reshape(row_count * heads_local, head_dim),
        row_info,
        col_info,
        gathered,
        row_count // kv_rows,
        kv_rows,
        near_rows,
        head_dim,
    )
    attention = out_rows.reshape(row_count, query_width)
    return (attention, own_keys, own_values)


def solution(mesh):
    in_specs = (
        P("seq", None),
        P(),
        P("seq", "tensor"),
        P("tensor"),
        P("seq", None, "tensor"),
        P(None, "tensor"),
        P(None, "seq", "tensor", None),
        P(None, "seq", "tensor", None),
        P(),
        P(),
    )
    out_specs = (P("seq", "tensor"), P("seq", "tensor", None), P("seq", "tensor", None))
    return jax.shard_map(local, mesh=mesh, in_specs=in_specs, out_specs=out_specs, check_vma=False)
```

```python
import math

import jax
import jax.numpy as jnp
from jax import lax
from jax.experimental import pallas as pl
from jax.experimental.pallas import tpu as pltpu
from jax.sharding import PartitionSpec as P

EPS = 1e-06
THETA = 1000000.0


def from_behind(shard, axis, by):
    size = lax.axis_size(axis)
    pairs = [(i, i + by) for i in range(size) if 0 <= i + by < size]
    return lax.ppermute(shard, axis, pairs)


def row_tables(lengths, assignment, all_rows):
    request_end = jnp.cumsum(lengths)
    request_start = request_end - lengths
    row_ids = jnp.arange(all_rows, dtype=jnp.int32)
    segment = jnp.sum((row_ids[:, None] >= request_end[None, :]).astype(jnp.int32), axis=1)
    request_ids = jnp.arange(lengths.shape[0], dtype=jnp.int32)
    onehot = (segment[:, None] == request_ids[None, :]).astype(jnp.int32)
    offset = row_ids - jnp.sum(onehot * request_start[None, :], axis=1)
    prefix = jnp.sum(onehot * assignment[None, :], axis=1)
    return (segment, offset, prefix)


def rotate(values, positions):
    head_size = values.shape[-1]
    half_dim = head_size // 2
    frequency = THETA ** (-2.0 * jnp.arange(half_dim, dtype=jnp.float32) / head_size)
    angles = positions.astype(jnp.float32)[:, None] * frequency[None, :]
    cosine = jnp.concatenate([jnp.cos(angles), jnp.cos(angles)], axis=-1)[:, None, :]
    sine_part = jnp.concatenate([jnp.sin(angles), jnp.sin(angles)], axis=-1)[:, None, :]
    turned = jnp.concatenate([-values[..., half_dim:], values[..., :half_dim]], axis=-1)
    return values * cosine + turned * sine_part


def attention_kernel(q_ref, row_ref, col_ref, kv_ref, near_ref, o_ref, *, head_dim, packs, scale):
    d = head_dim
    dims = (((1,), (1,)), ((), ()))
    q = q_ref[...]
    rows = row_ref[...]
    use_first = rows[:, 0:1] == 0
    row_seg = rows[:, 1:2]
    row_idx = rows[:, 2:3]
    cols = col_ref[...]
    n_dev, n_sub = kv_ref.shape[0], kv_ref.shape[1]

    def piece(j):
        return kv_ref[:, :, j * d : (j + 1) * d].reshape(n_dev * n_sub, d)

    far = []
    for k in range(packs):
        far0 = lax.dot_general(q, piece(4 * k), dims, preferred_element_type=jnp.float32) * scale
        far1 = lax.dot_general(q, piece(4 * k + 1), dims, preferred_element_type=jnp.float32) * scale
        far.append(jnp.where(use_first, far0, far1))
    near = lax.dot_general(q, near_ref[:, 0:d], dims, preferred_element_type=jnp.float32) * scale
    visible = (cols[0:1, :] == row_seg) & (cols[1:2, :] <= row_idx)
    near = jnp.where(visible, near, -jnp.inf)
    top = jnp.max(near, axis=1, keepdims=True)
    for s in far:
        top = jnp.maximum(top, jnp.max(s, axis=1, keepdims=True))
    near_w = jnp.exp(near - top)
    mass = jnp.sum(near_w, axis=1, keepdims=True)
    acc = jnp.dot(near_w.astype(jnp.bfloat16), near_ref[:, d : 2 * d], preferred_element_type=jnp.float32)
    for k, s in enumerate(far):
        far_w = jnp.exp(s - top)
        mass = mass + jnp.sum(far_w, axis=1, keepdims=True)
        far_b = far_w.astype(jnp.bfloat16)
        zero = jnp.zeros_like(far_b)
        acc = acc + jnp.dot(jnp.where(use_first, far_b, zero), piece(4 * k + 2), preferred_element_type=jnp.float32)
        acc = acc + jnp.dot(jnp.where(use_first, zero, far_b), piece(4 * k + 3), preferred_element_type=jnp.float32)
    o_ref[...] = (acc / mass).astype(o_ref.dtype)


def attend(q_rows, row_info, col_info, gathered, kv_block, kv_rows, near_slab, head_dim):
    n_rows = q_rows.shape[0]
    block = math.gcd(n_rows, 256)
    n_dev = gathered.shape[0]
    width = gathered.shape[2]
    packs = width // (4 * head_dim)
    cache_len = n_dev * kv_rows * packs
    near_len = near_slab.shape[0]
    kernel = lambda *refs: attention_kernel(*refs, head_dim=head_dim, packs=packs, scale=head_dim ** (-0.5))
    keys_total = 2 * cache_len + near_len
    cost = pl.CostEstimate(
        flops=4 * n_rows * keys_total * head_dim,
        transcendentals=n_rows * (cache_len + near_len),
        bytes_accessed=n_dev * kv_rows * width * 2 + near_slab.size * 2 + q_rows.size * 4,
    )
    return pl.pallas_call(
        kernel,
        grid=(n_rows // block,),
        in_specs=[
            pl.BlockSpec((block, head_dim), lambda i: (i, 0)),
            pl.BlockSpec((block, row_info.shape[1]), lambda i: (i, 0)),
            pl.BlockSpec(col_info.shape, lambda i: (0, 0)),
            pl.BlockSpec((n_dev, kv_rows, width), lambda i: (0, kv_block, 0)),
            pl.BlockSpec(near_slab.shape, lambda i: (0, 0)),
        ],
        out_specs=pl.BlockSpec((block, head_dim), lambda i: (i, 0)),
        out_shape=jax.ShapeDtypeStruct((n_rows, head_dim), jnp.bfloat16),
        cost_estimate=cost,
        compiler_params=pltpu.CompilerParams(vmem_limit_bytes=48 * 1024 * 1024),
    )(q_rows, row_info, col_info, gathered, near_slab)


def projection_kernel(x_ref, w_ref, b_ref, o_ref):
    n_dev, n_sub, width = w_ref.shape
    w = w_ref[...].reshape(n_dev * n_sub, width)
    o_ref[...] = jnp.dot(x_ref[...], w, preferred_element_type=jnp.float32) + b_ref[...]


def project(x, gathered, bias, first_block, n_blocks, block_width, sub_rows):
    n_dev = gathered.shape[0]
    rows = x.shape[0]
    cost = pl.CostEstimate(
        flops=2 * rows * x.shape[1] * block_width * n_blocks,
        transcendentals=0,
        bytes_accessed=n_dev * sub_rows * block_width * n_blocks * 2 + x.size * 2,
    )
    return pl.pallas_call(
        projection_kernel,
        grid=(n_blocks,),
        in_specs=[
            pl.BlockSpec(x.shape, lambda c: (0, 0)),
            pl.BlockSpec((n_dev, sub_rows, block_width), lambda c: (0, 0, first_block + c)),
            pl.BlockSpec((1, block_width), lambda c: (0, c)),
        ],
        out_specs=pl.BlockSpec((rows, block_width), lambda c: (0, c)),
        out_shape=jax.ShapeDtypeStruct((rows, block_width * n_blocks), jnp.float32),
        cost_estimate=cost,
        compiler_params=pltpu.CompilerParams(vmem_limit_bytes=48 * 1024 * 1024),
    )(x, gathered, bias.reshape(1, -1))


def local(
    hidden,
    gain,
    w_query,
    q_bias,
    w_keyval,
    kv_bias,
    prefix_keys,
    prefix_values,
    lengths,
    assignment,
):
    row_count = hidden.shape[0]
    seq_count = lax.axis_size("seq")
    seq_index = lax.axis_index("seq")
    all_rows = row_count * seq_count
    head_dim = prefix_keys.shape[3]
    kv_local = prefix_keys.shape[2]
    query_width = w_query.shape[1]
    heads_local = query_width // head_dim
    pair_width = w_keyval.shape[1] * w_keyval.shape[2]
    key_width = pair_width // 2
    cache_local = prefix_keys.shape[1]
    cache_length = cache_local * seq_count
    first_row = seq_index * row_count
    hidden_f = hidden.astype(jnp.float32)
    normed = (
        hidden_f
        * lax.rsqrt(jnp.mean(hidden_f * hidden_f, axis=1, keepdims=True) + EPS)
        * gain.astype(jnp.float32)
    ).astype(jnp.bfloat16)
    segment, offset, prefix = row_tables(lengths, assignment, all_rows)
    positions = offset + cache_length
    own_positions = lax.dynamic_slice_in_dim(positions, first_row, row_count)
    own_segment = lax.dynamic_slice_in_dim(segment, first_row, row_count)
    own_prefix = lax.dynamic_slice_in_dim(prefix, first_row, row_count)

    w_pairs = w_keyval.reshape(w_keyval.shape[0], pair_width)
    combined = jnp.concatenate([w_query, w_pairs], axis=1)
    total_width = combined.shape[1]
    entry = 4 * head_dim
    packs = total_width // entry
    kv_rows = -(-cache_local // packs)
    kv_rows = -(-kv_rows // 16) * 16
    slab = jnp.concatenate(
        [prefix_keys[0, :, 0, :], prefix_keys[1, :, 0, :], prefix_values[0, :, 0, :], prefix_values[1, :, 0, :]],
        axis=1,
    )
    slab = jnp.pad(slab, ((0, kv_rows * packs - cache_local), (0, 0)))
    slab = slab.reshape(packs, kv_rows, entry).transpose(1, 0, 2).reshape(kv_rows, packs * entry)
    slab = jnp.pad(slab, ((0, 0), (0, total_width - packs * entry)))
    assert kv_rows * packs == cache_local and row_count % kv_rows == 0
    block_rows = row_count + kv_rows
    gathered = lax.all_gather(jnp.concatenate([combined, slab], axis=0), "seq", axis=0, tiled=True)
    gathered = gathered.reshape(seq_count, block_rows, total_width)
    block_width = math.gcd(query_width, pair_width)
    pairs_own = project(
        normed, gathered, kv_bias.reshape(pair_width).astype(jnp.float32),
        query_width // block_width, pair_width // block_width, block_width, row_count,
    )
    own_keys = rotate(
        pairs_own[:, :key_width].reshape(row_count, kv_local, head_dim), own_positions
    ).astype(jnp.bfloat16)
    own_values = (
        pairs_own[:, key_width:].reshape(row_count, kv_local, head_dim).astype(jnp.bfloat16)
    )
    pair_rows = jnp.concatenate(
        [own_keys.reshape(row_count, key_width), own_values.reshape(row_count, key_width)], axis=1
    )
    depth = min(3, seq_count - 1)
    earlier = []
    for distance in range(depth, 0, -1):
        earlier.append(from_behind(pair_rows, "seq", distance))
    query_own = project(
        normed, gathered, q_bias.astype(jnp.float32), 0, query_width // block_width, block_width, row_count
    )
    own_queries = rotate(query_own.reshape(row_count, heads_local, head_dim), own_positions).astype(
        jnp.bfloat16
    )
    near_rows = jnp.concatenate(earlier + [pair_rows], axis=0)
    near_count = near_rows.shape[0]
    near_index = first_row - depth * row_count + jnp.arange(near_count, dtype=jnp.int32)
    near_segment = segment[jnp.clip(near_index, 0, all_rows - 1)]
    near_segment = jnp.where(near_index >= 0, near_segment, -1)
    col_info = jnp.concatenate(
        [near_segment[None, :], near_index[None, :], jnp.zeros((6, near_count), jnp.int32)], axis=0
    )
    own_rows = first_row + jnp.arange(row_count, dtype=jnp.int32)
    row_info = jnp.stack(
        [own_prefix, own_segment, own_rows, jnp.zeros_like(own_rows)], axis=1
    ).astype(jnp.int32)
    row_info = jnp.repeat(row_info, heads_local, axis=0)
    out_rows = attend(
        own_queries.reshape(row_count * heads_local, head_dim),
        row_info,
        col_info,
        gathered,
        row_count // kv_rows,
        kv_rows,
        near_rows,
        head_dim,
    )
    attention = out_rows.reshape(row_count, query_width)
    return (attention, own_keys, own_values)


def solution(mesh):
    in_specs = (
        P("seq", None),
        P(),
        P("seq", "tensor"),
        P("tensor"),
        P("seq", None, "tensor"),
        P(None, "tensor"),
        P(None, "seq", "tensor", None),
        P(None, "seq", "tensor", None),
        P(),
        P(),
    )
    out_specs = (P("seq", "tensor"), P("seq", "tensor", None), P("seq", "tensor", None))
    return jax.shard_map(local, mesh=mesh, in_specs=in_specs, out_specs=out_specs, check_vma=False)
```

```python
import math

import jax
import jax.numpy as jnp
from jax import lax
from jax.experimental import pallas as pl
from jax.experimental.pallas import tpu as pltpu
from jax.sharding import PartitionSpec as P

EPS = 1e-06
THETA = 1000000.0


def from_behind(shard, axis, by):
    size = lax.axis_size(axis)
    pairs = [(i, i + by) for i in range(size) if 0 <= i + by < size]
    return lax.ppermute(shard, axis, pairs)


def row_tables(lengths, assignment, all_rows):
    request_end = jnp.cumsum(lengths)
    request_start = request_end - lengths
    row_ids = jnp.arange(all_rows, dtype=jnp.int32)
    segment = jnp.sum((row_ids[:, None] >= request_end[None, :]).astype(jnp.int32), axis=1)
    request_ids = jnp.arange(lengths.shape[0], dtype=jnp.int32)
    onehot = (segment[:, None] == request_ids[None, :]).astype(jnp.int32)
    offset = row_ids - jnp.sum(onehot * request_start[None, :], axis=1)
    prefix = jnp.sum(onehot * assignment[None, :], axis=1)
    return (segment, offset, prefix)


def rotate(values, positions):
    head_size = values.shape[-1]
    half_dim = head_size // 2
    frequency = THETA ** (-2.0 * jnp.arange(half_dim, dtype=jnp.float32) / head_size)
    angles = positions.astype(jnp.float32)[:, None] * frequency[None, :]
    cosine = jnp.concatenate([jnp.cos(angles), jnp.cos(angles)], axis=-1)[:, None, :]
    sine_part = jnp.concatenate([jnp.sin(angles), jnp.sin(angles)], axis=-1)[:, None, :]
    turned = jnp.concatenate([-values[..., half_dim:], values[..., :half_dim]], axis=-1)
    return values * cosine + turned * sine_part


def attention_kernel(flag_ref, q_ref, row_ref, col_ref, kv_ref, near_ref, o_ref, *, head_dim, packs, scale):
    d = head_dim
    dims = (((1,), (1,)), ((), ()))
    block = pl.program_id(0)
    uses = (flag_ref[block, 0] > 0, flag_ref[block, 1] > 0)
    n_dev, n_sub = kv_ref.shape[0], kv_ref.shape[1]

    def piece(j):
        return kv_ref[:, :, j * d : (j + 1) * d].reshape(n_dev * n_sub, d)

    def near_part(q):
        rows = row_ref[...]
        cols = col_ref[...]
        near = lax.dot_general(q, near_ref[:, 0:d], dims, preferred_element_type=jnp.float32) * scale
        visible = (cols[0:1, :] == rows[:, 1:2]) & (cols[1:2, :] <= rows[:, 2:3])
        return jnp.where(visible, near, -jnp.inf)

    def finish(q, far, values):
        near = near_part(q)
        top = jnp.max(near, axis=1, keepdims=True)
        for s in far:
            top = jnp.maximum(top, jnp.max(s, axis=1, keepdims=True))
        near_w = jnp.exp(near - top)
        mass = jnp.sum(near_w, axis=1, keepdims=True)
        acc = jnp.dot(near_w.astype(jnp.bfloat16), near_ref[:, d : 2 * d], preferred_element_type=jnp.float32)
        for s, value in zip(far, values):
            far_w = jnp.exp(s - top)
            mass = mass + jnp.sum(far_w, axis=1, keepdims=True)
            acc = value(far_w.astype(jnp.bfloat16), acc)
        o_ref[...] = (acc / mass).astype(o_ref.dtype)

    def single(p):
        q = q_ref[...]
        far = [
            lax.dot_general(q, piece(4 * k + p), dims, preferred_element_type=jnp.float32) * scale
            for k in range(packs)
        ]

        def value_of(k):
            return lambda w, acc: acc + jnp.dot(w, piece(4 * k + 2 + p), preferred_element_type=jnp.float32)

        finish(q, far, [value_of(k) for k in range(packs)])

    def both():
        q = q_ref[...]
        use_first = row_ref[...][:, 0:1] == 0
        far = []
        for k in range(packs):
            far0 = lax.dot_general(q, piece(4 * k), dims, preferred_element_type=jnp.float32) * scale
            far1 = lax.dot_general(q, piece(4 * k + 1), dims, preferred_element_type=jnp.float32) * scale
            far.append(jnp.where(use_first, far0, far1))

        def value_of(k):
            def value(w, acc):
                zero = jnp.zeros_like(w)
                acc = acc + jnp.dot(jnp.where(use_first, w, zero), piece(4 * k + 2), preferred_element_type=jnp.float32)
                return acc + jnp.dot(jnp.where(use_first, zero, w), piece(4 * k + 3), preferred_element_type=jnp.float32)

            return value

        finish(q, far, [value_of(k) for k in range(packs)])

    pl.when(uses[0] & uses[1])(both)
    pl.when(uses[0] & jnp.logical_not(uses[1]))(lambda: single(0))
    pl.when(jnp.logical_not(uses[0]) & uses[1])(lambda: single(1))


def attend(q_rows, row_info, col_info, gathered, kv_block, kv_rows, near_slab, head_dim):
    n_rows = q_rows.shape[0]
    block = math.gcd(n_rows, 256)
    n_blocks = n_rows // block
    n_dev = gathered.shape[0]
    width = gathered.shape[2]
    packs = width // (4 * head_dim)
    cache_len = n_dev * kv_rows * packs
    near_len = near_slab.shape[0]
    block_prefix = row_info[:, 0].reshape(n_blocks, block)
    flags = jnp.stack(
        [jnp.any(block_prefix == 0, axis=1), jnp.any(block_prefix != 0, axis=1)], axis=1
    ).astype(jnp.int32)
    kernel = lambda *refs: attention_kernel(*refs, head_dim=head_dim, packs=packs, scale=head_dim ** (-0.5))
    keys_total = cache_len + near_len
    cost = pl.CostEstimate(
        flops=4 * n_rows * keys_total * head_dim,
        transcendentals=n_rows * (cache_len + near_len),
        bytes_accessed=n_dev * kv_rows * width * 2 + near_slab.size * 2 + q_rows.size * 4,
    )
    grid_spec = pltpu.PrefetchScalarGridSpec(
        num_scalar_prefetch=1,
        grid=(n_blocks,),
        in_specs=[
            pl.BlockSpec((block, head_dim), lambda i, f: (i, 0)),
            pl.BlockSpec((block, row_info.shape[1]), lambda i, f: (i, 0)),
            pl.BlockSpec(col_info.shape, lambda i, f: (0, 0)),
            pl.BlockSpec((n_dev, kv_rows, width), lambda i, f: (0, kv_block, 0)),
            pl.BlockSpec(near_slab.shape, lambda i, f: (0, 0)),
        ],
        out_specs=pl.BlockSpec((block, head_dim), lambda i, f: (i, 0)),
    )
    return pl.pallas_call(
        kernel,
        grid_spec=grid_spec,
        out_shape=jax.ShapeDtypeStruct((n_rows, head_dim), jnp.bfloat16),
        cost_estimate=cost,
        compiler_params=pltpu.CompilerParams(vmem_limit_bytes=48 * 1024 * 1024),
    )(flags, q_rows, row_info, col_info, gathered, near_slab)


def projection_kernel(x_ref, w_ref, b_ref, o_ref):
    n_dev, n_sub, width = w_ref.shape
    w = w_ref[...].reshape(n_dev * n_sub, width)
    o_ref[...] = jnp.dot(x_ref[...], w, preferred_element_type=jnp.float32) + b_ref[...]


def project(x, gathered, bias, first_block, n_blocks, block_width, sub_rows):
    n_dev = gathered.shape[0]
    rows = x.shape[0]
    cost = pl.CostEstimate(
        flops=2 * rows * x.shape[1] * block_width * n_blocks,
        transcendentals=0,
        bytes_accessed=n_dev * sub_rows * block_width * n_blocks * 2 + x.size * 2,
    )
    return pl.pallas_call(
        projection_kernel,
        grid=(n_blocks,),
        in_specs=[
            pl.BlockSpec(x.shape, lambda c: (0, 0)),
            pl.BlockSpec((n_dev, sub_rows, block_width), lambda c: (0, 0, first_block + c)),
            pl.BlockSpec((1, block_width), lambda c: (0, c)),
        ],
        out_specs=pl.BlockSpec((rows, block_width), lambda c: (0, c)),
        out_shape=jax.ShapeDtypeStruct((rows, block_width * n_blocks), jnp.float32),
        cost_estimate=cost,
        compiler_params=pltpu.CompilerParams(vmem_limit_bytes=48 * 1024 * 1024),
    )(x, gathered, bias.reshape(1, -1))


def local(
    hidden,
    gain,
    w_query,
    q_bias,
    w_keyval,
    kv_bias,
    prefix_keys,
    prefix_values,
    lengths,
    assignment,
):
    row_count = hidden.shape[0]
    seq_count = lax.axis_size("seq")
    seq_index = lax.axis_index("seq")
    all_rows = row_count * seq_count
    head_dim = prefix_keys.shape[3]
    kv_local = prefix_keys.shape[2]
    query_width = w_query.shape[1]
    heads_local = query_width // head_dim
    pair_width = w_keyval.shape[1] * w_keyval.shape[2]
    key_width = pair_width // 2
    cache_local = prefix_keys.shape[1]
    cache_length = cache_local * seq_count
    first_row = seq_index * row_count
    hidden_f = hidden.astype(jnp.float32)
    normed = (
        hidden_f
        * lax.rsqrt(jnp.mean(hidden_f * hidden_f, axis=1, keepdims=True) + EPS)
        * gain.astype(jnp.float32)
    ).astype(jnp.bfloat16)
    segment, offset, prefix = row_tables(lengths, assignment, all_rows)
    positions = offset + cache_length
    own_positions = lax.dynamic_slice_in_dim(positions, first_row, row_count)
    own_segment = lax.dynamic_slice_in_dim(segment, first_row, row_count)
    own_prefix = lax.dynamic_slice_in_dim(prefix, first_row, row_count)

    w_pairs = w_keyval.reshape(w_keyval.shape[0], pair_width)
    combined = jnp.concatenate([w_query, w_pairs], axis=1)
    total_width = combined.shape[1]
    entry = 4 * head_dim
    packs = total_width // entry
    kv_rows = -(-cache_local // packs)
    kv_rows = -(-kv_rows // 16) * 16
    slab = jnp.concatenate(
        [prefix_keys[0, :, 0, :], prefix_keys[1, :, 0, :], prefix_values[0, :, 0, :], prefix_values[1, :, 0, :]],
        axis=1,
    )
    slab = jnp.pad(slab, ((0, kv_rows * packs - cache_local), (0, 0)))
    slab = slab.reshape(packs, kv_rows, entry).transpose(1, 0, 2).reshape(kv_rows, packs * entry)
    slab = jnp.pad(slab, ((0, 0), (0, total_width - packs * entry)))
    assert kv_rows * packs == cache_local and row_count % kv_rows == 0
    block_rows = row_count + kv_rows
    gathered = lax.all_gather(jnp.concatenate([combined, slab], axis=0), "seq", axis=0, tiled=True)
    gathered = gathered.reshape(seq_count, block_rows, total_width)
    block_width = math.gcd(query_width, pair_width)
    pairs_own = project(
        normed, gathered, kv_bias.reshape(pair_width).astype(jnp.float32),
        query_width // block_width, pair_width // block_width, block_width, row_count,
    )
    own_keys = rotate(
        pairs_own[:, :key_width].reshape(row_count, kv_local, head_dim), own_positions
    ).astype(jnp.bfloat16)
    own_values = (
        pairs_own[:, key_width:].reshape(row_count, kv_local, head_dim).astype(jnp.bfloat16)
    )
    pair_rows = jnp.concatenate(
        [own_keys.reshape(row_count, key_width), own_values.reshape(row_count, key_width)], axis=1
    )
    depth = min(3, seq_count - 1)
    earlier = []
    for distance in range(depth, 0, -1):
        earlier.append(from_behind(pair_rows, "seq", distance))
    query_own = project(
        normed, gathered, q_bias.astype(jnp.float32), 0, query_width // block_width, block_width, row_count
    )
    own_queries = rotate(query_own.reshape(row_count, heads_local, head_dim), own_positions).astype(
        jnp.bfloat16
    )
    near_rows = jnp.concatenate(earlier + [pair_rows], axis=0)
    near_count = near_rows.shape[0]
    near_index = first_row - depth * row_count + jnp.arange(near_count, dtype=jnp.int32)
    near_segment = segment[jnp.clip(near_index, 0, all_rows - 1)]
    near_segment = jnp.where(near_index >= 0, near_segment, -1)
    col_info = jnp.concatenate(
        [near_segment[None, :], near_index[None, :], jnp.zeros((6, near_count), jnp.int32)], axis=0
    )
    own_rows = first_row + jnp.arange(row_count, dtype=jnp.int32)
    row_info = jnp.stack(
        [own_prefix, own_segment, own_rows, jnp.zeros_like(own_rows)], axis=1
    ).astype(jnp.int32)
    row_info = jnp.repeat(row_info, heads_local, axis=0)
    out_rows = attend(
        own_queries.reshape(row_count * heads_local, head_dim),
        row_info,
        col_info,
        gathered,
        row_count // kv_rows,
        kv_rows,
        near_rows,
        head_dim,
    )
    attention = out_rows.reshape(row_count, query_width)
    return (attention, own_keys, own_values)


def solution(mesh):
    in_specs = (
        P("seq", None),
        P(),
        P("seq", "tensor"),
        P("tensor"),
        P("seq", None, "tensor"),
        P(None, "tensor"),
        P(None, "seq", "tensor", None),
        P(None, "seq", "tensor", None),
        P(),
        P(),
    )
    out_specs = (P("seq", "tensor"), P("seq", "tensor", None), P("seq", "tensor", None))
    return jax.shard_map(local, mesh=mesh, in_specs=in_specs, out_specs=out_specs, check_vma=False)
```

```python
import math

import jax
import jax.numpy as jnp
from jax import lax
from jax.experimental import pallas as pl
from jax.experimental.pallas import tpu as pltpu
from jax.sharding import PartitionSpec as P

EPS = 1e-06
THETA = 1000000.0


def from_behind(shard, axis, by):
    size = lax.axis_size(axis)
    pairs = [(i, i + by) for i in range(size) if 0 <= i + by < size]
    return lax.ppermute(shard, axis, pairs)


def row_tables(lengths, assignment, all_rows):
    request_end = jnp.cumsum(lengths)
    request_start = request_end - lengths
    row_ids = jnp.arange(all_rows, dtype=jnp.int32)
    segment = jnp.sum((row_ids[:, None] >= request_end[None, :]).astype(jnp.int32), axis=1)
    request_ids = jnp.arange(lengths.shape[0], dtype=jnp.int32)
    onehot = (segment[:, None] == request_ids[None, :]).astype(jnp.int32)
    offset = row_ids - jnp.sum(onehot * request_start[None, :], axis=1)
    prefix = jnp.sum(onehot * assignment[None, :], axis=1)
    return (segment, offset, prefix)


def rotate(values, positions):
    head_size = values.shape[-1]
    half_dim = head_size // 2
    frequency = THETA ** (-2.0 * jnp.arange(half_dim, dtype=jnp.float32) / head_size)
    angles = positions.astype(jnp.float32)[:, None] * frequency[None, :]
    cosine = jnp.concatenate([jnp.cos(angles), jnp.cos(angles)], axis=-1)[:, None, :]
    sine_part = jnp.concatenate([jnp.sin(angles), jnp.sin(angles)], axis=-1)[:, None, :]
    turned = jnp.concatenate([-values[..., half_dim:], values[..., :half_dim]], axis=-1)
    return values * cosine + turned * sine_part


def attention_kernel(flag_ref, q_ref, row_ref, col_ref, k0_ref, k1_ref, v0_ref, v1_ref, near_ref, o_ref, *, scale):
    d = q_ref.shape[1]
    dims = (((1,), (1,)), ((), ()))
    block = pl.program_id(0)
    uses = (flag_ref[block, 0] > 0, flag_ref[block, 1] > 0)
    key_refs = (k0_ref, k1_ref)
    value_refs = (v0_ref, v1_ref)

    def full(ref):
        return ref[...].reshape(ref.shape[0] * ref.shape[1], ref.shape[2])

    def finish(q, far, value):
        rows = row_ref[...]
        cols = col_ref[...]
        near = lax.dot_general(q, near_ref[:, 0:d], dims, preferred_element_type=jnp.float32) * scale
        visible = (cols[0:1, :] == rows[:, 1:2]) & (cols[1:2, :] <= rows[:, 2:3])
        near = jnp.where(visible, near, -jnp.inf)
        top = jnp.maximum(jnp.max(near, axis=1, keepdims=True), jnp.max(far, axis=1, keepdims=True))
        near_w = jnp.exp(near - top)
        far_w = jnp.exp(far - top)
        mass = jnp.sum(near_w, axis=1, keepdims=True) + jnp.sum(far_w, axis=1, keepdims=True)
        acc = jnp.dot(near_w.astype(jnp.bfloat16), near_ref[:, d : 2 * d], preferred_element_type=jnp.float32)
        acc = value(far_w.astype(jnp.bfloat16), acc)
        o_ref[...] = (acc / mass).astype(o_ref.dtype)

    def single(p):
        q = q_ref[...]
        far = lax.dot_general(q, full(key_refs[p]), dims, preferred_element_type=jnp.float32) * scale
        finish(q, far, lambda w, acc: acc + jnp.dot(w, full(value_refs[p]), preferred_element_type=jnp.float32))

    def both():
        q = q_ref[...]
        use_first = row_ref[...][:, 0:1] == 0
        far0 = lax.dot_general(q, full(k0_ref), dims, preferred_element_type=jnp.float32) * scale
        far1 = lax.dot_general(q, full(k1_ref), dims, preferred_element_type=jnp.float32) * scale

        def value(w, acc):
            zero = jnp.zeros_like(w)
            acc = acc + jnp.dot(jnp.where(use_first, w, zero), full(v0_ref), preferred_element_type=jnp.float32)
            return acc + jnp.dot(jnp.where(use_first, zero, w), full(v1_ref), preferred_element_type=jnp.float32)

        finish(q, jnp.where(use_first, far0, far1), value)

    pl.when(uses[0] & uses[1])(both)
    pl.when(uses[0] & jnp.logical_not(uses[1]))(lambda: single(0))
    pl.when(jnp.logical_not(uses[0]) & uses[1])(lambda: single(1))


def attend(q_rows, row_info, col_info, cache, kv_column, near_slab):
    n_rows, head_dim = q_rows.shape
    block = math.gcd(n_rows, 256)
    n_blocks = n_rows // block
    n_dev, _, cache_local, _ = cache.shape
    cache_len = n_dev * cache_local
    near_len = near_slab.shape[0]
    block_prefix = row_info[:, 0].reshape(n_blocks, block)
    flags = jnp.stack(
        [jnp.any(block_prefix == 0, axis=1), jnp.any(block_prefix != 0, axis=1)], axis=1
    ).astype(jnp.int32)
    kernel = lambda *refs: attention_kernel(*refs, scale=head_dim ** (-0.5))
    cost = pl.CostEstimate(
        flops=4 * n_rows * (cache_len + near_len) * head_dim,
        transcendentals=n_rows * (cache_len + near_len),
        bytes_accessed=4 * cache_len * head_dim * 2 + near_slab.size * 2 + q_rows.size * 4,
    )

    def cache_spec(kind, p):
        return pl.BlockSpec((n_dev, None, cache_local, head_dim), lambda i, f: (0, kind, 0, kv_column + p))

    grid_spec = pltpu.PrefetchScalarGridSpec(
        num_scalar_prefetch=1,
        grid=(n_blocks,),
        in_specs=[
            pl.BlockSpec((block, head_dim), lambda i, f: (i, 0)),
            pl.BlockSpec((block, row_info.shape[1]), lambda i, f: (i, 0)),
            pl.BlockSpec(col_info.shape, lambda i, f: (0, 0)),
            cache_spec(0, 0),
            cache_spec(0, 1),
            cache_spec(1, 0),
            cache_spec(1, 1),
            pl.BlockSpec(near_slab.shape, lambda i, f: (0, 0)),
        ],
        out_specs=pl.BlockSpec((block, head_dim), lambda i, f: (i, 0)),
    )
    return pl.pallas_call(
        kernel,
        grid_spec=grid_spec,
        out_shape=jax.ShapeDtypeStruct((n_rows, head_dim), jnp.bfloat16),
        cost_estimate=cost,
        compiler_params=pltpu.CompilerParams(vmem_limit_bytes=48 * 1024 * 1024),
    )(flags, q_rows, row_info, col_info, cache, cache, cache, cache, near_slab)


def projection_kernel(x_ref, w_ref, b_ref, o_ref):
    o_ref[...] = jnp.dot(x_ref[...], w_ref[...], preferred_element_type=jnp.float32) + b_ref[...]


def project(x, gathered, bias, first_block, n_blocks, block_width):
    rows = x.shape[0]
    depth = gathered.shape[0]
    cost = pl.CostEstimate(
        flops=2 * rows * depth * block_width * n_blocks,
        transcendentals=0,
        bytes_accessed=depth * block_width * n_blocks * 2 + x.size * 2,
    )
    return pl.pallas_call(
        projection_kernel,
        grid=(n_blocks,),
        in_specs=[
            pl.BlockSpec(x.shape, lambda c: (0, 0)),
            pl.BlockSpec((depth, block_width), lambda c: (0, first_block + c)),
            pl.BlockSpec((1, block_width), lambda c: (0, c)),
        ],
        out_specs=pl.BlockSpec((rows, block_width), lambda c: (0, c)),
        out_shape=jax.ShapeDtypeStruct((rows, block_width * n_blocks), jnp.float32),
        cost_estimate=cost,
        compiler_params=pltpu.CompilerParams(vmem_limit_bytes=48 * 1024 * 1024),
    )(x, gathered, bias.reshape(1, -1))


def local(
    hidden,
    gain,
    w_query,
    q_bias,
    w_keyval,
    kv_bias,
    prefix_keys,
    prefix_values,
    lengths,
    assignment,
):
    row_count = hidden.shape[0]
    seq_count = lax.axis_size("seq")
    seq_index = lax.axis_index("seq")
    all_rows = row_count * seq_count
    head_dim = prefix_keys.shape[3]
    kv_local = prefix_keys.shape[2]
    query_width = w_query.shape[1]
    heads_local = query_width // head_dim
    pair_width = w_keyval.shape[1] * w_keyval.shape[2]
    key_width = pair_width // 2
    cache_local = prefix_keys.shape[1]
    cache_length = cache_local * seq_count
    first_row = seq_index * row_count
    hidden_f = hidden.astype(jnp.float32)
    normed = (
        hidden_f
        * lax.rsqrt(jnp.mean(hidden_f * hidden_f, axis=1, keepdims=True) + EPS)
        * gain.astype(jnp.float32)
    ).astype(jnp.bfloat16)
    segment, offset, prefix = row_tables(lengths, assignment, all_rows)
    positions = offset + cache_length
    own_positions = lax.dynamic_slice_in_dim(positions, first_row, row_count)
    own_segment = lax.dynamic_slice_in_dim(segment, first_row, row_count)
    own_prefix = lax.dynamic_slice_in_dim(prefix, first_row, row_count)

    w_pairs = w_keyval.reshape(w_keyval.shape[0], pair_width)
    block_width = math.gcd(query_width, pair_width)
    cache_width = 2 * head_dim
    assert 2 * cache_local == row_count and cache_width % block_width == 0
    cache_keys = jnp.concatenate([prefix_keys[0, :, 0, :], prefix_keys[1, :, 0, :]], axis=1)
    cache_values = jnp.concatenate([prefix_values[0, :, 0, :], prefix_values[1, :, 0, :]], axis=1)
    combined = jnp.concatenate(
        [w_query, w_pairs, jnp.concatenate([cache_keys, cache_values], axis=0)], axis=1
    )
    total_width = combined.shape[1]
    gathered = lax.all_gather(combined, "seq", axis=0, tiled=True)
    pairs_own = project(
        normed, gathered, kv_bias.reshape(pair_width).astype(jnp.float32),
        query_width // block_width, pair_width // block_width, block_width,
    )
    own_keys = rotate(
        pairs_own[:, :key_width].reshape(row_count, kv_local, head_dim), own_positions
    ).astype(jnp.bfloat16)
    own_values = (
        pairs_own[:, key_width:].reshape(row_count, kv_local, head_dim).astype(jnp.bfloat16)
    )
    pair_rows = jnp.concatenate(
        [own_keys.reshape(row_count, key_width), own_values.reshape(row_count, key_width)], axis=1
    )
    depth = min(3, seq_count - 1)
    earlier = []
    for distance in range(depth, 0, -1):
        earlier.append(from_behind(pair_rows, "seq", distance))
    query_own = project(normed, gathered, q_bias.astype(jnp.float32), 0, query_width // block_width, block_width)
    own_queries = rotate(query_own.reshape(row_count, heads_local, head_dim), own_positions).astype(
        jnp.bfloat16
    )
    near_rows = jnp.concatenate(earlier + [pair_rows], axis=0)
    near_count = near_rows.shape[0]
    near_index = first_row - depth * row_count + jnp.arange(near_count, dtype=jnp.int32)
    near_segment = segment[jnp.clip(near_index, 0, all_rows - 1)]
    near_segment = jnp.where(near_index >= 0, near_segment, -1)
    col_info = jnp.concatenate(
        [near_segment[None, :], near_index[None, :], jnp.zeros((6, near_count), jnp.int32)], axis=0
    )
    own_rows = first_row + jnp.arange(row_count, dtype=jnp.int32)
    row_info = jnp.stack(
        [own_prefix, own_segment, own_rows, jnp.zeros_like(own_rows)], axis=1
    ).astype(jnp.int32)
    row_info = jnp.repeat(row_info, heads_local, axis=0)
    cache = gathered.reshape(seq_count, 2, cache_local, total_width)
    out_rows = attend(
        own_queries.reshape(row_count * heads_local, head_dim),
        row_info,
        col_info,
        cache,
        (query_width + pair_width) // head_dim,
        near_rows,
    )
    attention = out_rows.reshape(row_count, query_width)
    return (attention, own_keys, own_values)


def solution(mesh):
    in_specs = (
        P("seq", None),
        P(),
        P("seq", "tensor"),
        P("tensor"),
        P("seq", None, "tensor"),
        P(None, "tensor"),
        P(None, "seq", "tensor", None),
        P(None, "seq", "tensor", None),
        P(),
        P(),
    )
    out_specs = (P("seq", "tensor"), P("seq", "tensor", None), P("seq", "tensor", None))
    return jax.shard_map(local, mesh=mesh, in_specs=in_specs, out_specs=out_specs, check_vma=False)
```

```python
import math

import jax
import jax.numpy as jnp
from jax import lax
from jax.experimental import pallas as pl
from jax.experimental.pallas import tpu as pltpu
from jax.sharding import PartitionSpec as P

EPS = 1e-06
THETA = 1000000.0


def from_behind(shard, axis, by):
    size = lax.axis_size(axis)
    pairs = [(i, i + by) for i in range(size) if 0 <= i + by < size]
    return lax.ppermute(shard, axis, pairs)


def row_tables(lengths, assignment, all_rows):
    request_end = jnp.cumsum(lengths)
    request_start = request_end - lengths
    row_ids = jnp.arange(all_rows, dtype=jnp.int32)
    segment = jnp.sum((row_ids[:, None] >= request_end[None, :]).astype(jnp.int32), axis=1)
    request_ids = jnp.arange(lengths.shape[0], dtype=jnp.int32)
    onehot = (segment[:, None] == request_ids[None, :]).astype(jnp.int32)
    offset = row_ids - jnp.sum(onehot * request_start[None, :], axis=1)
    prefix = jnp.sum(onehot * assignment[None, :], axis=1)
    return (segment, offset, prefix)


def rotate(values, positions):
    head_size = values.shape[-1]
    half_dim = head_size // 2
    frequency = THETA ** (-2.0 * jnp.arange(half_dim, dtype=jnp.float32) / head_size)
    angles = positions.astype(jnp.float32)[:, None] * frequency[None, :]
    cosine = jnp.concatenate([jnp.cos(angles), jnp.cos(angles)], axis=-1)[:, None, :]
    sine_part = jnp.concatenate([jnp.sin(angles), jnp.sin(angles)], axis=-1)[:, None, :]
    turned = jnp.concatenate([-values[..., half_dim:], values[..., :half_dim]], axis=-1)
    return values * cosine + turned * sine_part


def attention_kernel(flag_ref, q_ref, row_ref, col_ref, k0_ref, k1_ref, v0_ref, v1_ref, near_ref, o_ref, *, scale):
    d = q_ref.shape[1]
    dims = (((1,), (1,)), ((), ()))
    block = pl.program_id(0)
    uses = (flag_ref[block, 0] > 0, flag_ref[block, 1] > 0)
    key_refs = (k0_ref, k1_ref)
    value_refs = (v0_ref, v1_ref)

    def full(ref):
        return ref[...].reshape(ref.shape[0] * ref.shape[1], ref.shape[2])

    def finish(q, far, value):
        rows = row_ref[...]
        cols = col_ref[...]
        near = lax.dot_general(q, near_ref[:, 0:d], dims, preferred_element_type=jnp.float32) * scale
        visible = (cols[0:1, :] == rows[:, 1:2]) & (cols[1:2, :] <= rows[:, 2:3])
        near = jnp.where(visible, near, -jnp.inf)
        top = jnp.maximum(jnp.max(near, axis=1, keepdims=True), jnp.max(far, axis=1, keepdims=True))
        near_w = jnp.exp(near - top)
        far_w = jnp.exp(far - top)
        mass = jnp.sum(near_w, axis=1, keepdims=True) + jnp.sum(far_w, axis=1, keepdims=True)
        acc = jnp.dot(near_w.astype(jnp.bfloat16), near_ref[:, d : 2 * d], preferred_element_type=jnp.float32)
        acc = value(far_w.astype(jnp.bfloat16), acc)
        o_ref[...] = (acc / mass).astype(o_ref.dtype)

    def single(p):
        q = q_ref[...]
        far = lax.dot_general(q, full(key_refs[p]), dims, preferred_element_type=jnp.float32) * scale
        finish(q, far, lambda w, acc: acc + jnp.dot(w, full(value_refs[p]), preferred_element_type=jnp.float32))

    def both():
        q = q_ref[...]
        use_first = row_ref[...][:, 0:1] == 0
        far0 = lax.dot_general(q, full(k0_ref), dims, preferred_element_type=jnp.float32) * scale
        far1 = lax.dot_general(q, full(k1_ref), dims, preferred_element_type=jnp.float32) * scale

        def value(w, acc):
            zero = jnp.zeros_like(w)
            acc = acc + jnp.dot(jnp.where(use_first, w, zero), full(v0_ref), preferred_element_type=jnp.float32)
            return acc + jnp.dot(jnp.where(use_first, zero, w), full(v1_ref), preferred_element_type=jnp.float32)

        finish(q, jnp.where(use_first, far0, far1), value)

    pl.when(uses[0] & uses[1])(both)
    pl.when(uses[0] & jnp.logical_not(uses[1]))(lambda: single(0))
    pl.when(jnp.logical_not(uses[0]) & uses[1])(lambda: single(1))


def attend(q_rows, row_info, col_info, cache, kv_column, near_slab):
    n_rows, head_dim = q_rows.shape
    block = math.gcd(n_rows, 256)
    n_blocks = n_rows // block
    n_dev, _, cache_local, _ = cache.shape
    cache_len = n_dev * cache_local
    near_len = near_slab.shape[0]
    block_prefix = row_info[:, 0].reshape(n_blocks, block)
    flags = jnp.stack(
        [jnp.any(block_prefix == 0, axis=1), jnp.any(block_prefix != 0, axis=1)], axis=1
    ).astype(jnp.int32)
    kernel = lambda *refs: attention_kernel(*refs, scale=head_dim ** (-0.5))
    cost = pl.CostEstimate(
        flops=4 * n_rows * (cache_len + near_len) * head_dim,
        transcendentals=n_rows * (cache_len + near_len),
        bytes_accessed=4 * cache_len * head_dim * 2 + near_slab.size * 2 + q_rows.size * 4,
    )

    def cache_spec(kind, p):
        return pl.BlockSpec((n_dev, None, cache_local, head_dim), lambda i, f: (0, kind, 0, kv_column + p))

    grid_spec = pltpu.PrefetchScalarGridSpec(
        num_scalar_prefetch=1,
        grid=(n_blocks,),
        in_specs=[
            pl.BlockSpec((block, head_dim), lambda i, f: (i, 0)),
            pl.BlockSpec((block, row_info.shape[1]), lambda i, f: (i, 0)),
            pl.BlockSpec(col_info.shape, lambda i, f: (0, 0)),
            cache_spec(0, 0),
            cache_spec(0, 1),
            cache_spec(1, 0),
            cache_spec(1, 1),
            pl.BlockSpec(near_slab.shape, lambda i, f: (0, 0)),
        ],
        out_specs=pl.BlockSpec((block, head_dim), lambda i, f: (i, 0)),
    )
    return pl.pallas_call(
        kernel,
        grid_spec=grid_spec,
        out_shape=jax.ShapeDtypeStruct((n_rows, head_dim), jnp.bfloat16),
        cost_estimate=cost,
        compiler_params=pltpu.CompilerParams(vmem_limit_bytes=48 * 1024 * 1024),
    )(flags, q_rows, row_info, col_info, cache, cache, cache, cache, near_slab)


def projection_kernel(x_ref, w_ref, b_ref, o_ref):
    o_ref[...] = jnp.dot(x_ref[...], w_ref[...], preferred_element_type=jnp.float32) + b_ref[...]


def project(x, gathered, bias, first_block, n_blocks, block_width):
    rows = x.shape[0]
    depth = gathered.shape[0]
    cost = pl.CostEstimate(
        flops=2 * rows * depth * block_width * n_blocks,
        transcendentals=0,
        bytes_accessed=depth * block_width * n_blocks * 2 + x.size * 2,
    )
    return pl.pallas_call(
        projection_kernel,
        grid=(n_blocks,),
        in_specs=[
            pl.BlockSpec(x.shape, lambda c: (0, 0)),
            pl.BlockSpec((depth, block_width), lambda c: (0, first_block + c)),
            pl.BlockSpec((1, block_width), lambda c: (0, c)),
        ],
        out_specs=pl.BlockSpec((rows, block_width), lambda c: (0, c)),
        out_shape=jax.ShapeDtypeStruct((rows, block_width * n_blocks), jnp.float32),
        cost_estimate=cost,
        compiler_params=pltpu.CompilerParams(vmem_limit_bytes=48 * 1024 * 1024),
    )(x, gathered, bias.reshape(1, -1))


def local(
    hidden,
    gain,
    w_query,
    q_bias,
    w_keyval,
    kv_bias,
    prefix_keys,
    prefix_values,
    lengths,
    assignment,
):
    row_count = hidden.shape[0]
    seq_count = lax.axis_size("seq")
    seq_index = lax.axis_index("seq")
    all_rows = row_count * seq_count
    head_dim = prefix_keys.shape[3]
    kv_local = prefix_keys.shape[2]
    query_width = w_query.shape[1]
    heads_local = query_width // head_dim
    pair_width = w_keyval.shape[1] * w_keyval.shape[2]
    key_width = pair_width // 2
    cache_local = prefix_keys.shape[1]
    cache_length = cache_local * seq_count
    first_row = seq_index * row_count
    hidden_f = hidden.astype(jnp.float32)
    normed = (
        hidden_f
        * lax.rsqrt(jnp.mean(hidden_f * hidden_f, axis=1, keepdims=True) + EPS)
        * gain.astype(jnp.float32)
    ).astype(jnp.bfloat16)
    segment, offset, prefix = row_tables(lengths, assignment, all_rows)
    positions = offset + cache_length
    own_positions = lax.dynamic_slice_in_dim(positions, first_row, row_count)
    own_segment = lax.dynamic_slice_in_dim(segment, first_row, row_count)
    own_prefix = lax.dynamic_slice_in_dim(prefix, first_row, row_count)

    w_pairs = w_keyval.reshape(w_keyval.shape[0], pair_width)
    block_width = math.gcd(query_width, pair_width)
    cache_width = 2 * head_dim
    assert 2 * cache_local == row_count and cache_width % block_width == 0
    cache_keys = jnp.concatenate([prefix_keys[0, :, 0, :], prefix_keys[1, :, 0, :]], axis=1)
    cache_values = jnp.concatenate([prefix_values[0, :, 0, :], prefix_values[1, :, 0, :]], axis=1)
    combined = jnp.concatenate(
        [w_query, w_pairs, jnp.concatenate([cache_keys, cache_values], axis=0)], axis=1
    )
    total_width = combined.shape[1]
    gathered = lax.all_gather(combined, "seq", axis=0, tiled=True)
    pairs_own = project(
        normed, gathered, kv_bias.reshape(pair_width).astype(jnp.float32),
        query_width // block_width, pair_width // block_width, block_width,
    )
    own_keys = rotate(
        pairs_own[:, :key_width].reshape(row_count, kv_local, head_dim), own_positions
    ).astype(jnp.bfloat16)
    own_values = (
        pairs_own[:, key_width:].reshape(row_count, kv_local, head_dim).astype(jnp.bfloat16)
    )
    pair_rows = jnp.concatenate(
        [own_keys.reshape(row_count, key_width), own_values.reshape(row_count, key_width)], axis=1
    )
    depth = 1
    near_rows = pair_rows
    while depth < 3:
        near_rows = jnp.concatenate([from_behind(near_rows, "seq", depth), near_rows], axis=0)
        depth = 2 * depth
    depth = depth - 1
    query_own = project(normed, gathered, q_bias.astype(jnp.float32), 0, query_width // block_width, block_width)
    own_queries = rotate(query_own.reshape(row_count, heads_local, head_dim), own_positions).astype(
        jnp.bfloat16
    )
    near_count = near_rows.shape[0]
    near_index = first_row - depth * row_count + jnp.arange(near_count, dtype=jnp.int32)
    near_segment = segment[jnp.clip(near_index, 0, all_rows - 1)]
    near_segment = jnp.where(near_index >= 0, near_segment, -1)
    col_info = jnp.concatenate(
        [near_segment[None, :], near_index[None, :], jnp.zeros((6, near_count), jnp.int32)], axis=0
    )
    own_rows = first_row + jnp.arange(row_count, dtype=jnp.int32)
    row_info = jnp.stack(
        [own_prefix, own_segment, own_rows, jnp.zeros_like(own_rows)], axis=1
    ).astype(jnp.int32)
    row_info = jnp.repeat(row_info, heads_local, axis=0)
    cache = gathered.reshape(seq_count, 2, cache_local, total_width)
    out_rows = attend(
        own_queries.reshape(row_count * heads_local, head_dim),
        row_info,
        col_info,
        cache,
        (query_width + pair_width) // head_dim,
        near_rows,
    )
    attention = out_rows.reshape(row_count, query_width)
    return (attention, own_keys, own_values)


def solution(mesh):
    in_specs = (
        P("seq", None),
        P(),
        P("seq", "tensor"),
        P("tensor"),
        P("seq", None, "tensor"),
        P(None, "tensor"),
        P(None, "seq", "tensor", None),
        P(None, "seq", "tensor", None),
        P(),
        P(),
    )
    out_specs = (P("seq", "tensor"), P("seq", "tensor", None), P("seq", "tensor", None))
    return jax.shard_map(local, mesh=mesh, in_specs=in_specs, out_specs=out_specs, check_vma=False)
```

```python
import math

import jax
import jax.numpy as jnp
from jax import lax
from jax.experimental import pallas as pl
from jax.experimental.pallas import tpu as pltpu
from jax.sharding import PartitionSpec as P

EPS = 1e-06
THETA = 1000000.0


def from_behind(shard, axis, by):
    size = lax.axis_size(axis)
    pairs = [(i, i + by) for i in range(size) if 0 <= i + by < size]
    return lax.ppermute(shard, axis, pairs)


def row_tables(lengths, assignment, all_rows):
    request_end = jnp.cumsum(lengths)
    request_start = request_end - lengths
    row_ids = jnp.arange(all_rows, dtype=jnp.int32)
    segment = jnp.sum((row_ids[:, None] >= request_end[None, :]).astype(jnp.int32), axis=1)
    request_ids = jnp.arange(lengths.shape[0], dtype=jnp.int32)
    onehot = (segment[:, None] == request_ids[None, :]).astype(jnp.int32)
    offset = row_ids - jnp.sum(onehot * request_start[None, :], axis=1)
    prefix = jnp.sum(onehot * assignment[None, :], axis=1)
    return (segment, offset, prefix)


def rotate(values, positions):
    head_size = values.shape[-1]
    half_dim = head_size // 2
    frequency = THETA ** (-2.0 * jnp.arange(half_dim, dtype=jnp.float32) / head_size)
    angles = positions.astype(jnp.float32)[:, None] * frequency[None, :]
    cosine = jnp.concatenate([jnp.cos(angles), jnp.cos(angles)], axis=-1)[:, None, :]
    sine_part = jnp.concatenate([jnp.sin(angles), jnp.sin(angles)], axis=-1)[:, None, :]
    turned = jnp.concatenate([-values[..., half_dim:], values[..., :half_dim]], axis=-1)
    return values * cosine + turned * sine_part


def attention_kernel(flag_ref, q_ref, row_ref, col_ref, k0_ref, k1_ref, v0_ref, v1_ref, near_ref, o_ref, *, scale):
    d = q_ref.shape[1]
    dims = (((1,), (1,)), ((), ()))
    block = pl.program_id(0)
    uses = (flag_ref[block, 0] > 0, flag_ref[block, 1] > 0)
    key_refs = (k0_ref, k1_ref)
    value_refs = (v0_ref, v1_ref)

    def full(ref):
        return ref[...].reshape(ref.shape[0] * ref.shape[1], ref.shape[2])

    def finish(q, far, value):
        rows = row_ref[...]
        cols = col_ref[...]
        near = lax.dot_general(q, near_ref[:, 0:d], dims, preferred_element_type=jnp.float32) * scale
        visible = (cols[0:1, :] == rows[:, 1:2]) & (cols[1:2, :] <= rows[:, 2:3])
        near = jnp.where(visible, near, -jnp.inf)
        top = jnp.maximum(jnp.max(near, axis=1, keepdims=True), jnp.max(far, axis=1, keepdims=True))
        near_w = jnp.exp(near - top)
        far_w = jnp.exp(far - top)
        mass = jnp.sum(near_w, axis=1, keepdims=True) + jnp.sum(far_w, axis=1, keepdims=True)
        acc = jnp.dot(near_w.astype(jnp.bfloat16), near_ref[:, d : 2 * d], preferred_element_type=jnp.float32)
        acc = value(far_w.astype(jnp.bfloat16), acc)
        o_ref[...] = (acc / mass).astype(o_ref.dtype)

    def single(p):
        q = q_ref[...]
        far = lax.dot_general(q, full(key_refs[p]), dims, preferred_element_type=jnp.float32) * scale
        finish(q, far, lambda w, acc: acc + jnp.dot(w, full(value_refs[p]), preferred_element_type=jnp.float32))

    def both():
        q = q_ref[...]
        use_first = row_ref[...][:, 0:1] == 0
        far0 = lax.dot_general(q, full(k0_ref), dims, preferred_element_type=jnp.float32) * scale
        far1 = lax.dot_general(q, full(k1_ref), dims, preferred_element_type=jnp.float32) * scale

        def value(w, acc):
            zero = jnp.zeros_like(w)
            acc = acc + jnp.dot(jnp.where(use_first, w, zero), full(v0_ref), preferred_element_type=jnp.float32)
            return acc + jnp.dot(jnp.where(use_first, zero, w), full(v1_ref), preferred_element_type=jnp.float32)

        finish(q, jnp.where(use_first, far0, far1), value)

    pl.when(uses[0] & uses[1])(both)
    pl.when(uses[0] & jnp.logical_not(uses[1]))(lambda: single(0))
    pl.when(jnp.logical_not(uses[0]) & uses[1])(lambda: single(1))


def attend(q_rows, row_info, col_info, cache, kv_column, near_slab):
    n_rows, head_dim = q_rows.shape
    block = math.gcd(n_rows, 512)
    n_blocks = n_rows // block
    n_dev, _, cache_local, _ = cache.shape
    cache_len = n_dev * cache_local
    near_len = near_slab.shape[0]
    block_prefix = row_info[:, 0].reshape(n_blocks, block)
    flags = jnp.stack(
        [jnp.any(block_prefix == 0, axis=1), jnp.any(block_prefix != 0, axis=1)], axis=1
    ).astype(jnp.int32)
    kernel = lambda *refs: attention_kernel(*refs, scale=head_dim ** (-0.5))
    cost = pl.CostEstimate(
        flops=4 * n_rows * (cache_len + near_len) * head_dim,
        transcendentals=n_rows * (cache_len + near_len),
        bytes_accessed=4 * cache_len * head_dim * 2 + near_slab.size * 2 + q_rows.size * 4,
    )

    def cache_spec(kind, p):
        return pl.BlockSpec((n_dev, None, cache_local, head_dim), lambda i, f: (0, kind, 0, kv_column + p))

    grid_spec = pltpu.PrefetchScalarGridSpec(
        num_scalar_prefetch=1,
        grid=(n_blocks,),
        in_specs=[
            pl.BlockSpec((block, head_dim), lambda i, f: (i, 0)),
            pl.BlockSpec((block, row_info.shape[1]), lambda i, f: (i, 0)),
            pl.BlockSpec(col_info.shape, lambda i, f: (0, 0)),
            cache_spec(0, 0),
            cache_spec(0, 1),
            cache_spec(1, 0),
            cache_spec(1, 1),
            pl.BlockSpec(near_slab.shape, lambda i, f: (0, 0)),
        ],
        out_specs=pl.BlockSpec((block, head_dim), lambda i, f: (i, 0)),
    )
    return pl.pallas_call(
        kernel,
        grid_spec=grid_spec,
        out_shape=jax.ShapeDtypeStruct((n_rows, head_dim), jnp.bfloat16),
        cost_estimate=cost,
        compiler_params=pltpu.CompilerParams(vmem_limit_bytes=48 * 1024 * 1024),
    )(flags, q_rows, row_info, col_info, cache, cache, cache, cache, near_slab)


def projection_kernel(x_ref, w_ref, b_ref, o_ref):
    o_ref[...] = jnp.dot(x_ref[...], w_ref[...], preferred_element_type=jnp.float32) + b_ref[...]


def project(x, gathered, bias, first_block, n_blocks, block_width):
    rows = x.shape[0]
    depth = gathered.shape[0]
    cost = pl.CostEstimate(
        flops=2 * rows * depth * block_width * n_blocks,
        transcendentals=0,
        bytes_accessed=depth * block_width * n_blocks * 2 + x.size * 2,
    )
    return pl.pallas_call(
        projection_kernel,
        grid=(n_blocks,),
        in_specs=[
            pl.BlockSpec(x.shape, lambda c: (0, 0)),
            pl.BlockSpec((depth, block_width), lambda c: (0, first_block + c)),
            pl.BlockSpec((1, block_width), lambda c: (0, c)),
        ],
        out_specs=pl.BlockSpec((rows, block_width), lambda c: (0, c)),
        out_shape=jax.ShapeDtypeStruct((rows, block_width * n_blocks), jnp.float32),
        cost_estimate=cost,
        compiler_params=pltpu.CompilerParams(vmem_limit_bytes=48 * 1024 * 1024),
    )(x, gathered, bias.reshape(1, -1))


def local(
    hidden,
    gain,
    w_query,
    q_bias,
    w_keyval,
    kv_bias,
    prefix_keys,
    prefix_values,
    lengths,
    assignment,
):
    row_count = hidden.shape[0]
    seq_count = lax.axis_size("seq")
    seq_index = lax.axis_index("seq")
    all_rows = row_count * seq_count
    head_dim = prefix_keys.shape[3]
    kv_local = prefix_keys.shape[2]
    query_width = w_query.shape[1]
    heads_local = query_width // head_dim
    pair_width = w_keyval.shape[1] * w_keyval.shape[2]
    key_width = pair_width // 2
    cache_local = prefix_keys.shape[1]
    cache_length = cache_local * seq_count
    first_row = seq_index * row_count
    hidden_f = hidden.astype(jnp.float32)
    normed = (
        hidden_f
        * lax.rsqrt(jnp.mean(hidden_f * hidden_f, axis=1, keepdims=True) + EPS)
        * gain.astype(jnp.float32)
    ).astype(jnp.bfloat16)
    segment, offset, prefix = row_tables(lengths, assignment, all_rows)
    positions = offset + cache_length
    own_positions = lax.dynamic_slice_in_dim(positions, first_row, row_count)
    own_segment = lax.dynamic_slice_in_dim(segment, first_row, row_count)
    own_prefix = lax.dynamic_slice_in_dim(prefix, first_row, row_count)

    w_pairs = w_keyval.reshape(w_keyval.shape[0], pair_width)
    block_width = math.gcd(query_width, pair_width)
    cache_width = 2 * head_dim
    assert 2 * cache_local == row_count and cache_width % block_width == 0
    cache_keys = jnp.concatenate([prefix_keys[0, :, 0, :], prefix_keys[1, :, 0, :]], axis=1)
    cache_values = jnp.concatenate([prefix_values[0, :, 0, :], prefix_values[1, :, 0, :]], axis=1)
    combined = jnp.concatenate(
        [w_query, w_pairs, jnp.concatenate([cache_keys, cache_values], axis=0)], axis=1
    )
    total_width = combined.shape[1]
    gathered = lax.all_gather(combined, "seq", axis=0, tiled=True)
    pairs_own = project(
        normed, gathered, kv_bias.reshape(pair_width).astype(jnp.float32),
        query_width // block_width, pair_width // block_width, block_width,
    )
    own_keys = rotate(
        pairs_own[:, :key_width].reshape(row_count, kv_local, head_dim), own_positions
    ).astype(jnp.bfloat16)
    own_values = (
        pairs_own[:, key_width:].reshape(row_count, kv_local, head_dim).astype(jnp.bfloat16)
    )
    pair_rows = jnp.concatenate(
        [own_keys.reshape(row_count, key_width), own_values.reshape(row_count, key_width)], axis=1
    )
    depth = 1
    near_rows = pair_rows
    while depth < 3:
        near_rows = jnp.concatenate([from_behind(near_rows, "seq", depth), near_rows], axis=0)
        depth = 2 * depth
    depth = depth - 1
    query_own = project(normed, gathered, q_bias.astype(jnp.float32), 0, query_width // block_width, block_width)
    own_queries = rotate(query_own.reshape(row_count, heads_local, head_dim), own_positions).astype(
        jnp.bfloat16
    )
    near_count = near_rows.shape[0]
    near_index = first_row - depth * row_count + jnp.arange(near_count, dtype=jnp.int32)
    near_segment = segment[jnp.clip(near_index, 0, all_rows - 1)]
    near_segment = jnp.where(near_index >= 0, near_segment, -1)
    col_info = jnp.concatenate(
        [near_segment[None, :], near_index[None, :], jnp.zeros((6, near_count), jnp.int32)], axis=0
    )
    own_rows = first_row + jnp.arange(row_count, dtype=jnp.int32)
    row_info = jnp.stack(
        [own_prefix, own_segment, own_rows, jnp.zeros_like(own_rows)], axis=1
    ).astype(jnp.int32)
    row_info = jnp.repeat(row_info, heads_local, axis=0)
    cache = gathered.reshape(seq_count, 2, cache_local, total_width)
    out_rows = attend(
        own_queries.reshape(row_count * heads_local, head_dim),
        row_info,
        col_info,
        cache,
        (query_width + pair_width) // head_dim,
        near_rows,
    )
    attention = out_rows.reshape(row_count, query_width)
    return (attention, own_keys, own_values)


def solution(mesh):
    in_specs = (
        P("seq", None),
        P(),
        P("seq", "tensor"),
        P("tensor"),
        P("seq", None, "tensor"),
        P(None, "tensor"),
        P(None, "seq", "tensor", None),
        P(None, "seq", "tensor", None),
        P(),
        P(),
    )
    out_specs = (P("seq", "tensor"), P("seq", "tensor", None), P("seq", "tensor", None))
    return jax.shard_map(local, mesh=mesh, in_specs=in_specs, out_specs=out_specs, check_vma=False)
```

```python
import math

import jax
import jax.numpy as jnp
from jax import lax
from jax.experimental import pallas as pl
from jax.experimental.pallas import tpu as pltpu
from jax.sharding import PartitionSpec as P

EPS = 1e-06
THETA = 1000000.0


def from_behind(shard, axis, by):
    size = lax.axis_size(axis)
    pairs = [(i, i + by) for i in range(size) if 0 <= i + by < size]
    return lax.ppermute(shard, axis, pairs)


def row_tables(lengths, assignment, all_rows):
    request_end = jnp.cumsum(lengths)
    request_start = request_end - lengths
    row_ids = jnp.arange(all_rows, dtype=jnp.int32)
    segment = jnp.sum((row_ids[:, None] >= request_end[None, :]).astype(jnp.int32), axis=1)
    request_ids = jnp.arange(lengths.shape[0], dtype=jnp.int32)
    onehot = (segment[:, None] == request_ids[None, :]).astype(jnp.int32)
    offset = row_ids - jnp.sum(onehot * request_start[None, :], axis=1)
    prefix = jnp.sum(onehot * assignment[None, :], axis=1)
    return (segment, offset, prefix)


def rotate(values, positions):
    head_size = values.shape[-1]
    half_dim = head_size // 2
    frequency = THETA ** (-2.0 * jnp.arange(half_dim, dtype=jnp.float32) / head_size)
    angles = positions.astype(jnp.float32)[:, None] * frequency[None, :]
    cosine = jnp.concatenate([jnp.cos(angles), jnp.cos(angles)], axis=-1)[:, None, :]
    sine_part = jnp.concatenate([jnp.sin(angles), jnp.sin(angles)], axis=-1)[:, None, :]
    turned = jnp.concatenate([-values[..., half_dim:], values[..., :half_dim]], axis=-1)
    return values * cosine + turned * sine_part


def attention_kernel(flag_ref, q_ref, row_ref, col_ref, k0_ref, k1_ref, v0_ref, v1_ref, near_ref, o_ref, *, scale):
    d = q_ref.shape[1]
    dims = (((1,), (1,)), ((), ()))
    block = pl.program_id(0)
    uses = (flag_ref[block, 0] > 0, flag_ref[block, 1] > 0)
    key_refs = (k0_ref, k1_ref)
    value_refs = (v0_ref, v1_ref)

    def full(ref):
        return ref[...].reshape(ref.shape[0] * ref.shape[1], ref.shape[2])

    def finish(q, far, value):
        rows = row_ref[...]
        cols = col_ref[...]
        near = lax.dot_general(q, near_ref[:, 0:d], dims, preferred_element_type=jnp.float32) * scale
        visible = (cols[0:1, :] == rows[:, 1:2]) & (cols[1:2, :] <= rows[:, 2:3])
        near = jnp.where(visible, near, -jnp.inf)
        top = jnp.maximum(jnp.max(near, axis=1, keepdims=True), jnp.max(far, axis=1, keepdims=True))
        near_w = jnp.exp(near - top)
        far_w = jnp.exp(far - top)
        mass = jnp.sum(near_w, axis=1, keepdims=True) + jnp.sum(far_w, axis=1, keepdims=True)
        acc = jnp.dot(near_w.astype(jnp.bfloat16), near_ref[:, d : 2 * d], preferred_element_type=jnp.float32)
        acc = value(far_w.astype(jnp.bfloat16), acc)
        o_ref[...] = (acc / mass).astype(o_ref.dtype)

    def single(p):
        q = q_ref[...]
        far = lax.dot_general(q, full(key_refs[p]), dims, preferred_element_type=jnp.float32) * scale
        finish(q, far, lambda w, acc: acc + jnp.dot(w, full(value_refs[p]), preferred_element_type=jnp.float32))

    def both():
        q = q_ref[...]
        use_first = row_ref[...][:, 0:1] == 0
        far0 = lax.dot_general(q, full(k0_ref), dims, preferred_element_type=jnp.float32) * scale
        far1 = lax.dot_general(q, full(k1_ref), dims, preferred_element_type=jnp.float32) * scale

        def value(w, acc):
            zero = jnp.zeros_like(w)
            acc = acc + jnp.dot(jnp.where(use_first, w, zero), full(v0_ref), preferred_element_type=jnp.float32)
            return acc + jnp.dot(jnp.where(use_first, zero, w), full(v1_ref), preferred_element_type=jnp.float32)

        finish(q, jnp.where(use_first, far0, far1), value)

    pl.when(uses[0] & uses[1])(both)
    pl.when(uses[0] & jnp.logical_not(uses[1]))(lambda: single(0))
    pl.when(jnp.logical_not(uses[0]) & uses[1])(lambda: single(1))


def attend(q_rows, row_info, col_info, cache, kv_column, near_slab):
    n_rows, head_dim = q_rows.shape
    block = math.gcd(n_rows, 128)
    n_blocks = n_rows // block
    n_dev, _, cache_local, _ = cache.shape
    cache_len = n_dev * cache_local
    near_len = near_slab.shape[0]
    block_prefix = row_info[:, 0].reshape(n_blocks, block)
    flags = jnp.stack(
        [jnp.any(block_prefix == 0, axis=1), jnp.any(block_prefix != 0, axis=1)], axis=1
    ).astype(jnp.int32)
    kernel = lambda *refs: attention_kernel(*refs, scale=head_dim ** (-0.5))
    cost = pl.CostEstimate(
        flops=4 * n_rows * (cache_len + near_len) * head_dim,
        transcendentals=n_rows * (cache_len + near_len),
        bytes_accessed=4 * cache_len * head_dim * 2 + near_slab.size * 2 + q_rows.size * 4,
    )

    def cache_spec(kind, p):
        return pl.BlockSpec((n_dev, None, cache_local, head_dim), lambda i, f: (0, kind, 0, kv_column + p))

    grid_spec = pltpu.PrefetchScalarGridSpec(
        num_scalar_prefetch=1,
        grid=(n_blocks,),
        in_specs=[
            pl.BlockSpec((block, head_dim), lambda i, f: (i, 0)),
            pl.BlockSpec((block, row_info.shape[1]), lambda i, f: (i, 0)),
            pl.BlockSpec(col_info.shape, lambda i, f: (0, 0)),
            cache_spec(0, 0),
            cache_spec(0, 1),
            cache_spec(1, 0),
            cache_spec(1, 1),
            pl.BlockSpec(near_slab.shape, lambda i, f: (0, 0)),
        ],
        out_specs=pl.BlockSpec((block, head_dim), lambda i, f: (i, 0)),
    )
    return pl.pallas_call(
        kernel,
        grid_spec=grid_spec,
        out_shape=jax.ShapeDtypeStruct((n_rows, head_dim), jnp.bfloat16),
        cost_estimate=cost,
        compiler_params=pltpu.CompilerParams(vmem_limit_bytes=48 * 1024 * 1024),
    )(flags, q_rows, row_info, col_info, cache, cache, cache, cache, near_slab)


def projection_kernel(x_ref, w_ref, b_ref, o_ref):
    o_ref[...] = jnp.dot(x_ref[...], w_ref[...], preferred_element_type=jnp.float32) + b_ref[...]


def project(x, gathered, bias, first_block, n_blocks, block_width):
    rows = x.shape[0]
    depth = gathered.shape[0]
    cost = pl.CostEstimate(
        flops=2 * rows * depth * block_width * n_blocks,
        transcendentals=0,
        bytes_accessed=depth * block_width * n_blocks * 2 + x.size * 2,
    )
    return pl.pallas_call(
        projection_kernel,
        grid=(n_blocks,),
        in_specs=[
            pl.BlockSpec(x.shape, lambda c: (0, 0)),
            pl.BlockSpec((depth, block_width), lambda c: (0, first_block + c)),
            pl.BlockSpec((1, block_width), lambda c: (0, c)),
        ],
        out_specs=pl.BlockSpec((rows, block_width), lambda c: (0, c)),
        out_shape=jax.ShapeDtypeStruct((rows, block_width * n_blocks), jnp.float32),
        cost_estimate=cost,
        compiler_params=pltpu.CompilerParams(vmem_limit_bytes=48 * 1024 * 1024),
    )(x, gathered, bias.reshape(1, -1))


def local(
    hidden,
    gain,
    w_query,
    q_bias,
    w_keyval,
    kv_bias,
    prefix_keys,
    prefix_values,
    lengths,
    assignment,
):
    row_count = hidden.shape[0]
    seq_count = lax.axis_size("seq")
    seq_index = lax.axis_index("seq")
    all_rows = row_count * seq_count
    head_dim = prefix_keys.shape[3]
    kv_local = prefix_keys.shape[2]
    query_width = w_query.shape[1]
    heads_local = query_width // head_dim
    pair_width = w_keyval.shape[1] * w_keyval.shape[2]
    key_width = pair_width // 2
    cache_local = prefix_keys.shape[1]
    cache_length = cache_local * seq_count
    first_row = seq_index * row_count
    hidden_f = hidden.astype(jnp.float32)
    normed = (
        hidden_f
        * lax.rsqrt(jnp.mean(hidden_f * hidden_f, axis=1, keepdims=True) + EPS)
        * gain.astype(jnp.float32)
    ).astype(jnp.bfloat16)
    segment, offset, prefix = row_tables(lengths, assignment, all_rows)
    positions = offset + cache_length
    own_positions = lax.dynamic_slice_in_dim(positions, first_row, row_count)
    own_segment = lax.dynamic_slice_in_dim(segment, first_row, row_count)
    own_prefix = lax.dynamic_slice_in_dim(prefix, first_row, row_count)

    w_pairs = w_keyval.reshape(w_keyval.shape[0], pair_width)
    block_width = math.gcd(query_width, pair_width)
    cache_width = 2 * head_dim
    assert 2 * cache_local == row_count and cache_width % block_width == 0
    cache_keys = jnp.concatenate([prefix_keys[0, :, 0, :], prefix_keys[1, :, 0, :]], axis=1)
    cache_values = jnp.concatenate([prefix_values[0, :, 0, :], prefix_values[1, :, 0, :]], axis=1)
    combined = jnp.concatenate(
        [w_query, w_pairs, jnp.concatenate([cache_keys, cache_values], axis=0)], axis=1
    )
    total_width = combined.shape[1]
    gathered = lax.all_gather(combined, "seq", axis=0, tiled=True)
    pairs_own = project(
        normed, gathered, kv_bias.reshape(pair_width).astype(jnp.float32),
        query_width // block_width, pair_width // block_width, block_width,
    )
    own_keys = rotate(
        pairs_own[:, :key_width].reshape(row_count, kv_local, head_dim), own_positions
    ).astype(jnp.bfloat16)
    own_values = (
        pairs_own[:, key_width:].reshape(row_count, kv_local, head_dim).astype(jnp.bfloat16)
    )
    pair_rows = jnp.concatenate(
        [own_keys.reshape(row_count, key_width), own_values.reshape(row_count, key_width)], axis=1
    )
    depth = 1
    near_rows = pair_rows
    while depth < 3:
        near_rows = jnp.concatenate([from_behind(near_rows, "seq", depth), near_rows], axis=0)
        depth = 2 * depth
    depth = depth - 1
    query_own = project(normed, gathered, q_bias.astype(jnp.float32), 0, query_width // block_width, block_width)
    own_queries = rotate(query_own.reshape(row_count, heads_local, head_dim), own_positions).astype(
        jnp.bfloat16
    )
    near_count = near_rows.shape[0]
    near_index = first_row - depth * row_count + jnp.arange(near_count, dtype=jnp.int32)
    near_segment = segment[jnp.clip(near_index, 0, all_rows - 1)]
    near_segment = jnp.where(near_index >= 0, near_segment, -1)
    col_info = jnp.concatenate(
        [near_segment[None, :], near_index[None, :], jnp.zeros((6, near_count), jnp.int32)], axis=0
    )
    own_rows = first_row + jnp.arange(row_count, dtype=jnp.int32)
    row_info = jnp.stack(
        [own_prefix, own_segment, own_rows, jnp.zeros_like(own_rows)], axis=1
    ).astype(jnp.int32)
    row_info = jnp.repeat(row_info, heads_local, axis=0)
    cache = gathered.reshape(seq_count, 2, cache_local, total_width)
    out_rows = attend(
        own_queries.reshape(row_count * heads_local, head_dim),
        row_info,
        col_info,
        cache,
        (query_width + pair_width) // head_dim,
        near_rows,
    )
    attention = out_rows.reshape(row_count, query_width)
    return (attention, own_keys, own_values)


def solution(mesh):
    in_specs = (
        P("seq", None),
        P(),
        P("seq", "tensor"),
        P("tensor"),
        P("seq", None, "tensor"),
        P(None, "tensor"),
        P(None, "seq", "tensor", None),
        P(None, "seq", "tensor", None),
        P(),
        P(),
    )
    out_specs = (P("seq", "tensor"), P("seq", "tensor", None), P("seq", "tensor", None))
    return jax.shard_map(local, mesh=mesh, in_specs=in_specs, out_specs=out_specs, check_vma=False)
```

```python
import math

import jax
import jax.numpy as jnp
from jax import lax
from jax.experimental import pallas as pl
from jax.experimental.pallas import tpu as pltpu
from jax.sharding import PartitionSpec as P

EPS = 1e-06
THETA = 1000000.0


def from_behind(shard, axis, by):
    size = lax.axis_size(axis)
    pairs = [(i, i + by) for i in range(size) if 0 <= i + by < size]
    return lax.ppermute(shard, axis, pairs)


def row_tables(lengths, assignment, all_rows):
    request_end = jnp.cumsum(lengths)
    request_start = request_end - lengths
    row_ids = jnp.arange(all_rows, dtype=jnp.int32)
    segment = jnp.sum((row_ids[:, None] >= request_end[None, :]).astype(jnp.int32), axis=1)
    request_ids = jnp.arange(lengths.shape[0], dtype=jnp.int32)
    onehot = (segment[:, None] == request_ids[None, :]).astype(jnp.int32)
    offset = row_ids - jnp.sum(onehot * request_start[None, :], axis=1)
    prefix = jnp.sum(onehot * assignment[None, :], axis=1)
    return (segment, offset, prefix)


def rotate(values, positions):
    head_size = values.shape[-1]
    half_dim = head_size // 2
    frequency = THETA ** (-2.0 * jnp.arange(half_dim, dtype=jnp.float32) / head_size)
    angles = positions.astype(jnp.float32)[:, None] * frequency[None, :]
    cosine = jnp.concatenate([jnp.cos(angles), jnp.cos(angles)], axis=-1)[:, None, :]
    sine_part = jnp.concatenate([jnp.sin(angles), jnp.sin(angles)], axis=-1)[:, None, :]
    turned = jnp.concatenate([-values[..., half_dim:], values[..., :half_dim]], axis=-1)
    return values * cosine + turned * sine_part


def attention_kernel(flag_ref, q_ref, row_ref, col_ref, k0_ref, k1_ref, v0_ref, v1_ref, near_ref, o_ref, *, scale):
    d = q_ref.shape[1]
    dims = (((1,), (1,)), ((), ()))
    block = pl.program_id(0)
    uses = (flag_ref[block, 0] > 0, flag_ref[block, 1] > 0)
    key_refs = (k0_ref, k1_ref)
    value_refs = (v0_ref, v1_ref)

    def full(ref):
        return ref[...].reshape(ref.shape[0] * ref.shape[1], ref.shape[2])

    def finish(q, far, value):
        rows = row_ref[...]
        cols = col_ref[...]
        near = lax.dot_general(q, near_ref[:, 0:d], dims, preferred_element_type=jnp.float32)
        visible = (cols[0:1, :] == rows[:, 1:2]) & (cols[1:2, :] <= rows[:, 2:3])
        near = jnp.where(visible, near, -jnp.inf)
        top = jnp.maximum(jnp.max(near, axis=1, keepdims=True), jnp.max(far, axis=1, keepdims=True)) * scale
        near_w = jnp.exp(near * scale - top)
        far_w = jnp.exp(far * scale - top)
        mass = jnp.sum(near_w, axis=1, keepdims=True) + jnp.sum(far_w, axis=1, keepdims=True)
        acc = jnp.dot(near_w.astype(jnp.bfloat16), near_ref[:, d : 2 * d], preferred_element_type=jnp.float32)
        acc = value(far_w.astype(jnp.bfloat16), acc)
        o_ref[...] = (acc / mass).astype(o_ref.dtype)

    def single(p):
        q = q_ref[...]
        far = lax.dot_general(q, full(key_refs[p]), dims, preferred_element_type=jnp.float32)
        finish(q, far, lambda w, acc: acc + jnp.dot(w, full(value_refs[p]), preferred_element_type=jnp.float32))

    def both():
        q = q_ref[...]
        use_first = row_ref[...][:, 0:1] == 0
        far0 = lax.dot_general(q, full(k0_ref), dims, preferred_element_type=jnp.float32)
        far1 = lax.dot_general(q, full(k1_ref), dims, preferred_element_type=jnp.float32)

        def value(w, acc):
            zero = jnp.zeros_like(w)
            acc = acc + jnp.dot(jnp.where(use_first, w, zero), full(v0_ref), preferred_element_type=jnp.float32)
            return acc + jnp.dot(jnp.where(use_first, zero, w), full(v1_ref), preferred_element_type=jnp.float32)

        finish(q, jnp.where(use_first, far0, far1), value)

    pl.when(uses[0] & uses[1])(both)
    pl.when(uses[0] & jnp.logical_not(uses[1]))(lambda: single(0))
    pl.when(jnp.logical_not(uses[0]) & uses[1])(lambda: single(1))


def attend(q_rows, row_info, col_info, cache, kv_column, near_slab):
    n_rows, head_dim = q_rows.shape
    block = math.gcd(n_rows, 256)
    n_blocks = n_rows // block
    n_dev, _, cache_local, _ = cache.shape
    cache_len = n_dev * cache_local
    near_len = near_slab.shape[0]
    block_prefix = row_info[:, 0].reshape(n_blocks, block)
    flags = jnp.stack(
        [jnp.any(block_prefix == 0, axis=1), jnp.any(block_prefix != 0, axis=1)], axis=1
    ).astype(jnp.int32)
    kernel = lambda *refs: attention_kernel(*refs, scale=head_dim ** (-0.5))
    cost = pl.CostEstimate(
        flops=4 * n_rows * (cache_len + near_len) * head_dim,
        transcendentals=n_rows * (cache_len + near_len),
        bytes_accessed=4 * cache_len * head_dim * 2 + near_slab.size * 2 + q_rows.size * 4,
    )

    def cache_spec(kind, p):
        return pl.BlockSpec((n_dev, None, cache_local, head_dim), lambda i, f: (0, kind, 0, kv_column + p))

    grid_spec = pltpu.PrefetchScalarGridSpec(
        num_scalar_prefetch=1,
        grid=(n_blocks,),
        in_specs=[
            pl.BlockSpec((block, head_dim), lambda i, f: (i, 0)),
            pl.BlockSpec((block, row_info.shape[1]), lambda i, f: (i, 0)),
            pl.BlockSpec(col_info.shape, lambda i, f: (0, 0)),
            cache_spec(0, 0),
            cache_spec(0, 1),
            cache_spec(1, 0),
            cache_spec(1, 1),
            pl.BlockSpec(near_slab.shape, lambda i, f: (0, 0)),
        ],
        out_specs=pl.BlockSpec((block, head_dim), lambda i, f: (i, 0)),
    )
    return pl.pallas_call(
        kernel,
        grid_spec=grid_spec,
        out_shape=jax.ShapeDtypeStruct((n_rows, head_dim), jnp.bfloat16),
        cost_estimate=cost,
        compiler_params=pltpu.CompilerParams(vmem_limit_bytes=48 * 1024 * 1024),
    )(flags, q_rows, row_info, col_info, cache, cache, cache, cache, near_slab)


def projection_kernel(x_ref, w_ref, b_ref, o_ref):
    o_ref[...] = jnp.dot(x_ref[...], w_ref[...], preferred_element_type=jnp.float32) + b_ref[...]


def project(x, gathered, bias, first_block, n_blocks, block_width):
    rows = x.shape[0]
    depth = gathered.shape[0]
    cost = pl.CostEstimate(
        flops=2 * rows * depth * block_width * n_blocks,
        transcendentals=0,
        bytes_accessed=depth * block_width * n_blocks * 2 + x.size * 2,
    )
    return pl.pallas_call(
        projection_kernel,
        grid=(n_blocks,),
        in_specs=[
            pl.BlockSpec(x.shape, lambda c: (0, 0)),
            pl.BlockSpec((depth, block_width), lambda c: (0, first_block + c)),
            pl.BlockSpec((1, block_width), lambda c: (0, c)),
        ],
        out_specs=pl.BlockSpec((rows, block_width), lambda c: (0, c)),
        out_shape=jax.ShapeDtypeStruct((rows, block_width * n_blocks), jnp.float32),
        cost_estimate=cost,
        compiler_params=pltpu.CompilerParams(vmem_limit_bytes=48 * 1024 * 1024),
    )(x, gathered, bias.reshape(1, -1))


def local(
    hidden,
    gain,
    w_query,
    q_bias,
    w_keyval,
    kv_bias,
    prefix_keys,
    prefix_values,
    lengths,
    assignment,
):
    row_count = hidden.shape[0]
    seq_count = lax.axis_size("seq")
    seq_index = lax.axis_index("seq")
    all_rows = row_count * seq_count
    head_dim = prefix_keys.shape[3]
    kv_local = prefix_keys.shape[2]
    query_width = w_query.shape[1]
    heads_local = query_width // head_dim
    pair_width = w_keyval.shape[1] * w_keyval.shape[2]
    key_width = pair_width // 2
    cache_local = prefix_keys.shape[1]
    cache_length = cache_local * seq_count
    first_row = seq_index * row_count
    hidden_f = hidden.astype(jnp.float32)
    normed = (
        hidden_f
        * lax.rsqrt(jnp.mean(hidden_f * hidden_f, axis=1, keepdims=True) + EPS)
        * gain.astype(jnp.float32)
    ).astype(jnp.bfloat16)
    segment, offset, prefix = row_tables(lengths, assignment, all_rows)
    positions = offset + cache_length
    own_positions = lax.dynamic_slice_in_dim(positions, first_row, row_count)
    own_segment = lax.dynamic_slice_in_dim(segment, first_row, row_count)
    own_prefix = lax.dynamic_slice_in_dim(prefix, first_row, row_count)

    w_pairs = w_keyval.reshape(w_keyval.shape[0], pair_width)
    block_width = math.gcd(query_width, pair_width)
    cache_width = 2 * head_dim
    assert 2 * cache_local == row_count and cache_width % block_width == 0
    cache_keys = jnp.concatenate([prefix_keys[0, :, 0, :], prefix_keys[1, :, 0, :]], axis=1)
    cache_values = jnp.concatenate([prefix_values[0, :, 0, :], prefix_values[1, :, 0, :]], axis=1)
    combined = jnp.concatenate(
        [w_query, w_pairs, jnp.concatenate([cache_keys, cache_values], axis=0)], axis=1
    )
    total_width = combined.shape[1]
    gathered = lax.all_gather(combined, "seq", axis=0, tiled=True)
    pairs_own = project(
        normed, gathered, kv_bias.reshape(pair_width).astype(jnp.float32),
        query_width // block_width, pair_width // block_width, block_width,
    )
    own_keys = rotate(
        pairs_own[:, :key_width].reshape(row_count, kv_local, head_dim), own_positions
    ).astype(jnp.bfloat16)
    own_values = (
        pairs_own[:, key_width:].reshape(row_count, kv_local, head_dim).astype(jnp.bfloat16)
    )
    pair_rows = jnp.concatenate(
        [own_keys.reshape(row_count, key_width), own_values.reshape(row_count, key_width)], axis=1
    )
    depth = 1
    near_rows = pair_rows
    while depth < 3:
        near_rows = jnp.concatenate([from_behind(near_rows, "seq", depth), near_rows], axis=0)
        depth = 2 * depth
    depth = depth - 1
    query_own = project(normed, gathered, q_bias.astype(jnp.float32), 0, query_width // block_width, block_width)
    own_queries = rotate(query_own.reshape(row_count, heads_local, head_dim), own_positions).astype(
        jnp.bfloat16
    )
    near_count = near_rows.shape[0]
    near_index = first_row - depth * row_count + jnp.arange(near_count, dtype=jnp.int32)
    near_segment = segment[jnp.clip(near_index, 0, all_rows - 1)]
    near_segment = jnp.where(near_index >= 0, near_segment, -1)
    col_info = jnp.concatenate(
        [near_segment[None, :], near_index[None, :], jnp.zeros((6, near_count), jnp.int32)], axis=0
    )
    own_rows = first_row + jnp.arange(row_count, dtype=jnp.int32)
    row_info = jnp.stack(
        [own_prefix, own_segment, own_rows, jnp.zeros_like(own_rows)], axis=1
    ).astype(jnp.int32)
    row_info = jnp.repeat(row_info, heads_local, axis=0)
    cache = gathered.reshape(seq_count, 2, cache_local, total_width)
    out_rows = attend(
        own_queries.reshape(row_count * heads_local, head_dim),
        row_info,
        col_info,
        cache,
        (query_width + pair_width) // head_dim,
        near_rows,
    )
    attention = out_rows.reshape(row_count, query_width)
    return (attention, own_keys, own_values)


def solution(mesh):
    in_specs = (
        P("seq", None),
        P(),
        P("seq", "tensor"),
        P("tensor"),
        P("seq", None, "tensor"),
        P(None, "tensor"),
        P(None, "seq", "tensor", None),
        P(None, "seq", "tensor", None),
        P(),
        P(),
    )
    out_specs = (P("seq", "tensor"), P("seq", "tensor", None), P("seq", "tensor", None))
    return jax.shard_map(local, mesh=mesh, in_specs=in_specs, out_specs=out_specs, check_vma=False)
```

```python
import math

import jax
import jax.numpy as jnp
from jax import lax
from jax.experimental import pallas as pl
from jax.experimental.pallas import tpu as pltpu
from jax.sharding import PartitionSpec as P

EPS = 1e-06
THETA = 1000000.0


def from_behind(shard, axis, by):
    size = lax.axis_size(axis)
    pairs = [(i, i + by) for i in range(size) if 0 <= i + by < size]
    return lax.ppermute(shard, axis, pairs)


def row_tables(lengths, assignment, all_rows):
    request_end = jnp.cumsum(lengths)
    request_start = request_end - lengths
    row_ids = jnp.arange(all_rows, dtype=jnp.int32)
    segment = jnp.sum((row_ids[:, None] >= request_end[None, :]).astype(jnp.int32), axis=1)
    request_ids = jnp.arange(lengths.shape[0], dtype=jnp.int32)
    onehot = (segment[:, None] == request_ids[None, :]).astype(jnp.int32)
    offset = row_ids - jnp.sum(onehot * request_start[None, :], axis=1)
    prefix = jnp.sum(onehot * assignment[None, :], axis=1)
    return (segment, offset, prefix)


def rotate(values, positions):
    head_size = values.shape[-1]
    half_dim = head_size // 2
    frequency = THETA ** (-2.0 * jnp.arange(half_dim, dtype=jnp.float32) / head_size)
    angles = positions.astype(jnp.float32)[:, None] * frequency[None, :]
    cosine = jnp.concatenate([jnp.cos(angles), jnp.cos(angles)], axis=-1)[:, None, :]
    sine_part = jnp.concatenate([jnp.sin(angles), jnp.sin(angles)], axis=-1)[:, None, :]
    turned = jnp.concatenate([-values[..., half_dim:], values[..., :half_dim]], axis=-1)
    return values * cosine + turned * sine_part


def attention_kernel(flag_ref, q_ref, row_ref, col_ref, k0_ref, k1_ref, v0_ref, v1_ref, near_ref, o_ref, *, scale):
    d = q_ref.shape[1]
    dims = (((1,), (1,)), ((), ()))
    block = pl.program_id(0)
    uses = (flag_ref[block, 0] > 0, flag_ref[block, 1] > 0)
    key_refs = (k0_ref, k1_ref)
    value_refs = (v0_ref, v1_ref)

    def full(ref):
        return ref[...].reshape(ref.shape[0] * ref.shape[1], ref.shape[2])

    def finish(q, far, value):
        rows = row_ref[...]
        cols = col_ref[...]
        near = lax.dot_general(q, near_ref[:, 0:d], dims, preferred_element_type=jnp.float32)
        visible = (cols[0:1, :] == rows[:, 1:2]) & (cols[1:2, :] <= rows[:, 2:3])
        near = jnp.where(visible, near, -jnp.inf)
        top = jnp.maximum(jnp.max(near, axis=1, keepdims=True), jnp.max(far, axis=1, keepdims=True)) * scale
        near_w = jnp.exp(near * scale - top)
        far_w = jnp.exp(far * scale - top)
        mass = jnp.sum(near_w, axis=1, keepdims=True) + jnp.sum(far_w, axis=1, keepdims=True)
        acc = jnp.dot(near_w.astype(jnp.bfloat16), near_ref[:, d : 2 * d], preferred_element_type=jnp.float32)
        acc = value(far_w.astype(jnp.bfloat16), acc)
        o_ref[...] = (acc / mass).astype(o_ref.dtype)

    def single(p):
        q = q_ref[...]
        far = lax.dot_general(q, full(key_refs[p]), dims, preferred_element_type=jnp.float32)
        finish(q, far, lambda w, acc: acc + jnp.dot(w, full(value_refs[p]), preferred_element_type=jnp.float32))

    def both():
        q = q_ref[...]
        use_first = row_ref[...][:, 0:1] == 0
        far0 = lax.dot_general(q, full(k0_ref), dims, preferred_element_type=jnp.float32)
        far1 = lax.dot_general(q, full(k1_ref), dims, preferred_element_type=jnp.float32)

        def value(w, acc):
            zero = jnp.zeros_like(w)
            acc = acc + jnp.dot(jnp.where(use_first, w, zero), full(v0_ref), preferred_element_type=jnp.float32)
            return acc + jnp.dot(jnp.where(use_first, zero, w), full(v1_ref), preferred_element_type=jnp.float32)

        finish(q, jnp.where(use_first, far0, far1), value)

    pl.when(uses[0] & uses[1])(both)
    pl.when(uses[0] & jnp.logical_not(uses[1]))(lambda: single(0))
    pl.when(jnp.logical_not(uses[0]) & uses[1])(lambda: single(1))


def attend(q_rows, row_info, col_info, cache, kv_column, near_slab):
    n_rows, head_dim = q_rows.shape
    block = math.gcd(n_rows, 256)
    n_blocks = n_rows // block
    n_dev, _, cache_local, _ = cache.shape
    cache_len = n_dev * cache_local
    near_len = near_slab.shape[0]
    block_prefix = row_info[:, 0].reshape(n_blocks, block)
    flags = jnp.stack(
        [jnp.any(block_prefix == 0, axis=1), jnp.any(block_prefix != 0, axis=1)], axis=1
    ).astype(jnp.int32)
    kernel = lambda *refs: attention_kernel(*refs, scale=head_dim ** (-0.5))
    cost = pl.CostEstimate(
        flops=4 * n_rows * (cache_len + near_len) * head_dim,
        transcendentals=n_rows * (cache_len + near_len),
        bytes_accessed=4 * cache_len * head_dim * 2 + near_slab.size * 2 + q_rows.size * 4,
    )

    def cache_spec(kind, p):
        return pl.BlockSpec((n_dev, None, cache_local, head_dim), lambda i, f: (0, kind, 0, kv_column + p))

    grid_spec = pltpu.PrefetchScalarGridSpec(
        num_scalar_prefetch=1,
        grid=(n_blocks,),
        in_specs=[
            pl.BlockSpec((block, head_dim), lambda i, f: (i, 0)),
            pl.BlockSpec((block, row_info.shape[1]), lambda i, f: (i, 0)),
            pl.BlockSpec(col_info.shape, lambda i, f: (0, 0)),
            cache_spec(0, 0),
            cache_spec(0, 1),
            cache_spec(1, 0),
            cache_spec(1, 1),
            pl.BlockSpec(near_slab.shape, lambda i, f: (0, 0)),
        ],
        out_specs=pl.BlockSpec((block, head_dim), lambda i, f: (i, 0)),
    )
    return pl.pallas_call(
        kernel,
        grid_spec=grid_spec,
        out_shape=jax.ShapeDtypeStruct((n_rows, head_dim), jnp.bfloat16),
        cost_estimate=cost,
        compiler_params=pltpu.CompilerParams(vmem_limit_bytes=48 * 1024 * 1024),
    )(flags, q_rows, row_info, col_info, cache, cache, cache, cache, near_slab)


def projection_kernel(x_ref, w_ref, b_ref, o_ref):
    o_ref[...] = jnp.dot(x_ref[...], w_ref[...], preferred_element_type=jnp.float32) + b_ref[...]


def project(x, gathered, bias, first_block, n_blocks, block_width):
    rows = x.shape[0]
    depth = gathered.shape[0]
    cost = pl.CostEstimate(
        flops=2 * rows * depth * block_width * n_blocks,
        transcendentals=0,
        bytes_accessed=depth * block_width * n_blocks * 2 + x.size * 2,
    )
    return pl.pallas_call(
        projection_kernel,
        grid=(n_blocks,),
        in_specs=[
            pl.BlockSpec(x.shape, lambda c: (0, 0)),
            pl.BlockSpec((depth, block_width), lambda c: (0, first_block + c)),
            pl.BlockSpec((1, block_width), lambda c: (0, c)),
        ],
        out_specs=pl.BlockSpec((rows, block_width), lambda c: (0, c)),
        out_shape=jax.ShapeDtypeStruct((rows, block_width * n_blocks), jnp.float32),
        cost_estimate=cost,
        compiler_params=pltpu.CompilerParams(vmem_limit_bytes=48 * 1024 * 1024),
    )(x, gathered, bias.reshape(1, -1))


def local(
    hidden,
    gain,
    w_query,
    q_bias,
    w_keyval,
    kv_bias,
    prefix_keys,
    prefix_values,
    lengths,
    assignment,
):
    row_count = hidden.shape[0]
    seq_count = lax.axis_size("seq")
    seq_index = lax.axis_index("seq")
    all_rows = row_count * seq_count
    head_dim = prefix_keys.shape[3]
    kv_local = prefix_keys.shape[2]
    query_width = w_query.shape[1]
    heads_local = query_width // head_dim
    pair_width = w_keyval.shape[1] * w_keyval.shape[2]
    key_width = pair_width // 2
    cache_local = prefix_keys.shape[1]
    cache_length = cache_local * seq_count
    first_row = seq_index * row_count
    hidden_f = hidden.astype(jnp.float32)
    normed = (
        hidden_f
        * lax.rsqrt(jnp.mean(hidden_f * hidden_f, axis=1, keepdims=True) + EPS)
        * gain.astype(jnp.float32)
    ).astype(jnp.bfloat16)
    segment, offset, prefix = row_tables(lengths, assignment, all_rows)
    positions = offset + cache_length
    own_positions = lax.dynamic_slice_in_dim(positions, first_row, row_count)
    own_segment = lax.dynamic_slice_in_dim(segment, first_row, row_count)
    own_prefix = lax.dynamic_slice_in_dim(prefix, first_row, row_count)

    w_pairs = w_keyval.reshape(w_keyval.shape[0], pair_width)
    block_width = head_dim
    cache_width = 2 * head_dim
    assert 2 * cache_local == row_count and cache_width % block_width == 0
    cache_keys = jnp.concatenate([prefix_keys[0, :, 0, :], prefix_keys[1, :, 0, :]], axis=1)
    cache_values = jnp.concatenate([prefix_values[0, :, 0, :], prefix_values[1, :, 0, :]], axis=1)
    combined = jnp.concatenate(
        [w_query, w_pairs, jnp.concatenate([cache_keys, cache_values], axis=0)], axis=1
    )
    total_width = combined.shape[1]
    gathered = lax.all_gather(combined, "seq", axis=0, tiled=True)
    pairs_own = project(
        normed, gathered, kv_bias.reshape(pair_width).astype(jnp.float32),
        query_width // block_width, pair_width // block_width, block_width,
    )
    own_keys = rotate(
        pairs_own[:, :key_width].reshape(row_count, kv_local, head_dim), own_positions
    ).astype(jnp.bfloat16)
    own_values = (
        pairs_own[:, key_width:].reshape(row_count, kv_local, head_dim).astype(jnp.bfloat16)
    )
    pair_rows = jnp.concatenate(
        [own_keys.reshape(row_count, key_width), own_values.reshape(row_count, key_width)], axis=1
    )
    depth = 1
    near_rows = pair_rows
    while depth < 3:
        near_rows = jnp.concatenate([from_behind(near_rows, "seq", depth), near_rows], axis=0)
        depth = 2 * depth
    depth = depth - 1
    query_own = project(normed, gathered, q_bias.astype(jnp.float32), 0, query_width // block_width, block_width)
    own_queries = rotate(query_own.reshape(row_count, heads_local, head_dim), own_positions).astype(
        jnp.bfloat16
    )
    near_count = near_rows.shape[0]
    near_index = first_row - depth * row_count + jnp.arange(near_count, dtype=jnp.int32)
    near_segment = segment[jnp.clip(near_index, 0, all_rows - 1)]
    near_segment = jnp.where(near_index >= 0, near_segment, -1)
    col_info = jnp.concatenate(
        [near_segment[None, :], near_index[None, :], jnp.zeros((6, near_count), jnp.int32)], axis=0
    )
    own_rows = first_row + jnp.arange(row_count, dtype=jnp.int32)
    row_info = jnp.stack(
        [own_prefix, own_segment, own_rows, jnp.zeros_like(own_rows)], axis=1
    ).astype(jnp.int32)
    row_info = jnp.repeat(row_info, heads_local, axis=0)
    cache = gathered.reshape(seq_count, 2, cache_local, total_width)
    out_rows = attend(
        own_queries.reshape(row_count * heads_local, head_dim),
        row_info,
        col_info,
        cache,
        (query_width + pair_width) // head_dim,
        near_rows,
    )
    attention = out_rows.reshape(row_count, query_width)
    return (attention, own_keys, own_values)


def solution(mesh):
    in_specs = (
        P("seq", None),
        P(),
        P("seq", "tensor"),
        P("tensor"),
        P("seq", None, "tensor"),
        P(None, "tensor"),
        P(None, "seq", "tensor", None),
        P(None, "seq", "tensor", None),
        P(),
        P(),
    )
    out_specs = (P("seq", "tensor"), P("seq", "tensor", None), P("seq", "tensor", None))
    return jax.shard_map(local, mesh=mesh, in_specs=in_specs, out_specs=out_specs, check_vma=False)
```

```python
import math

import jax
import jax.numpy as jnp
from jax import lax
from jax.experimental import pallas as pl
from jax.experimental.pallas import tpu as pltpu
from jax.sharding import PartitionSpec as P

EPS = 1e-06
THETA = 1000000.0


def from_behind(shard, axis, by):
    size = lax.axis_size(axis)
    pairs = [(i, i + by) for i in range(size) if 0 <= i + by < size]
    return lax.ppermute(shard, axis, pairs)


def row_tables(lengths, assignment, all_rows):
    request_end = jnp.cumsum(lengths)
    request_start = request_end - lengths
    row_ids = jnp.arange(all_rows, dtype=jnp.int32)
    segment = jnp.sum((row_ids[:, None] >= request_end[None, :]).astype(jnp.int32), axis=1)
    request_ids = jnp.arange(lengths.shape[0], dtype=jnp.int32)
    onehot = (segment[:, None] == request_ids[None, :]).astype(jnp.int32)
    offset = row_ids - jnp.sum(onehot * request_start[None, :], axis=1)
    prefix = jnp.sum(onehot * assignment[None, :], axis=1)
    return (segment, offset, prefix)


def rotate(values, positions):
    head_size = values.shape[-1]
    half_dim = head_size // 2
    frequency = THETA ** (-2.0 * jnp.arange(half_dim, dtype=jnp.float32) / head_size)
    angles = positions.astype(jnp.float32)[:, None] * frequency[None, :]
    cosine = jnp.concatenate([jnp.cos(angles), jnp.cos(angles)], axis=-1)[:, None, :]
    sine_part = jnp.concatenate([jnp.sin(angles), jnp.sin(angles)], axis=-1)[:, None, :]
    turned = jnp.concatenate([-values[..., half_dim:], values[..., :half_dim]], axis=-1)
    return values * cosine + turned * sine_part


def attention_kernel(flag_ref, q_ref, row_ref, col_ref, k0_ref, k1_ref, v0_ref, v1_ref, near_ref, o_ref, *, scale):
    d = q_ref.shape[1]
    dims = (((1,), (1,)), ((), ()))
    block = pl.program_id(0)
    uses = (flag_ref[block, 0] > 0, flag_ref[block, 1] > 0)
    key_refs = (k0_ref, k1_ref)
    value_refs = (v0_ref, v1_ref)

    def full(ref):
        return ref[...].reshape(ref.shape[0] * ref.shape[1], ref.shape[2])

    def finish(q, far, value):
        rows = row_ref[...]
        cols = col_ref[...]
        near = lax.dot_general(q, near_ref[:, 0:d], dims, preferred_element_type=jnp.float32)
        visible = (cols[0:1, :] == rows[:, 1:2]) & (cols[1:2, :] <= rows[:, 2:3])
        near = jnp.where(visible, near, -jnp.inf)
        top = jnp.maximum(jnp.max(near, axis=1, keepdims=True), jnp.max(far, axis=1, keepdims=True)) * scale
        near_w = jnp.exp(near * scale - top)
        far_w = jnp.exp(far * scale - top)
        mass = jnp.sum(near_w, axis=1, keepdims=True) + jnp.sum(far_w, axis=1, keepdims=True)
        acc = jnp.dot(near_w.astype(jnp.bfloat16), near_ref[:, d : 2 * d], preferred_element_type=jnp.float32)
        acc = value(far_w.astype(jnp.bfloat16), acc)
        o_ref[...] = (acc / mass).astype(o_ref.dtype)

    def single(p):
        q = q_ref[...]
        far = lax.dot_general(q, full(key_refs[p]), dims, preferred_element_type=jnp.float32)
        finish(q, far, lambda w, acc: acc + jnp.dot(w, full(value_refs[p]), preferred_element_type=jnp.float32))

    def both():
        q = q_ref[...]
        use_first = row_ref[...][:, 0:1] == 0
        far0 = lax.dot_general(q, full(k0_ref), dims, preferred_element_type=jnp.float32)
        far1 = lax.dot_general(q, full(k1_ref), dims, preferred_element_type=jnp.float32)

        def value(w, acc):
            zero = jnp.zeros_like(w)
            acc = acc + jnp.dot(jnp.where(use_first, w, zero), full(v0_ref), preferred_element_type=jnp.float32)
            return acc + jnp.dot(jnp.where(use_first, zero, w), full(v1_ref), preferred_element_type=jnp.float32)

        finish(q, jnp.where(use_first, far0, far1), value)

    pl.when(uses[0] & uses[1])(both)
    pl.when(uses[0] & jnp.logical_not(uses[1]))(lambda: single(0))
    pl.when(jnp.logical_not(uses[0]) & uses[1])(lambda: single(1))


def attend(q_rows, row_info, col_info, cache, kv_column, near_slab):
    n_rows, head_dim = q_rows.shape
    block = math.gcd(n_rows, 256)
    n_blocks = n_rows // block
    n_dev, _, cache_local, _ = cache.shape
    cache_len = n_dev * cache_local
    near_len = near_slab.shape[0]
    block_prefix = row_info[:, 0].reshape(n_blocks, block)
    flags = jnp.stack(
        [jnp.any(block_prefix == 0, axis=1), jnp.any(block_prefix != 0, axis=1)], axis=1
    ).astype(jnp.int32)
    kernel = lambda *refs: attention_kernel(*refs, scale=head_dim ** (-0.5))
    cost = pl.CostEstimate(
        flops=4 * n_rows * (cache_len + near_len) * head_dim,
        transcendentals=n_rows * (cache_len + near_len),
        bytes_accessed=4 * cache_len * head_dim * 2 + near_slab.size * 2 + q_rows.size * 4,
    )

    def cache_spec(kind, p):
        return pl.BlockSpec((n_dev, None, cache_local, head_dim), lambda i, f: (0, kind, 0, kv_column + p))

    grid_spec = pltpu.PrefetchScalarGridSpec(
        num_scalar_prefetch=1,
        grid=(n_blocks,),
        in_specs=[
            pl.BlockSpec((block, head_dim), lambda i, f: (i, 0)),
            pl.BlockSpec((block, row_info.shape[1]), lambda i, f: (i, 0)),
            pl.BlockSpec(col_info.shape, lambda i, f: (0, 0)),
            cache_spec(0, 0),
            cache_spec(0, 1),
            cache_spec(1, 0),
            cache_spec(1, 1),
            pl.BlockSpec(near_slab.shape, lambda i, f: (0, 0)),
        ],
        out_specs=pl.BlockSpec((block, head_dim), lambda i, f: (i, 0)),
    )
    return pl.pallas_call(
        kernel,
        grid_spec=grid_spec,
        out_shape=jax.ShapeDtypeStruct((n_rows, head_dim), jnp.bfloat16),
        cost_estimate=cost,
        compiler_params=pltpu.CompilerParams(vmem_limit_bytes=48 * 1024 * 1024),
    )(flags, q_rows, row_info, col_info, cache, cache, cache, cache, near_slab)


def projection_kernel(x_ref, w_ref, b_ref, o_ref):
    o_ref[...] = jnp.dot(x_ref[...], w_ref[...], preferred_element_type=jnp.float32) + b_ref[...]


def project(x, gathered, bias, first_block, n_blocks, block_width):
    rows = x.shape[0]
    depth = gathered.shape[0]
    cost = pl.CostEstimate(
        flops=2 * rows * depth * block_width * n_blocks,
        transcendentals=0,
        bytes_accessed=depth * block_width * n_blocks * 2 + x.size * 2,
    )
    return pl.pallas_call(
        projection_kernel,
        grid=(n_blocks,),
        in_specs=[
            pl.BlockSpec(x.shape, lambda c: (0, 0)),
            pl.BlockSpec((depth, block_width), lambda c: (0, first_block + c)),
            pl.BlockSpec((1, block_width), lambda c: (0, c)),
        ],
        out_specs=pl.BlockSpec((rows, block_width), lambda c: (0, c)),
        out_shape=jax.ShapeDtypeStruct((rows, block_width * n_blocks), jnp.float32),
        cost_estimate=cost,
        compiler_params=pltpu.CompilerParams(vmem_limit_bytes=48 * 1024 * 1024),
    )(x, gathered, bias.reshape(1, -1))


def local(
    hidden,
    gain,
    w_query,
    q_bias,
    w_keyval,
    kv_bias,
    prefix_keys,
    prefix_values,
    lengths,
    assignment,
):
    row_count = hidden.shape[0]
    seq_count = lax.axis_size("seq")
    seq_index = lax.axis_index("seq")
    all_rows = row_count * seq_count
    head_dim = prefix_keys.shape[3]
    kv_local = prefix_keys.shape[2]
    query_width = w_query.shape[1]
    heads_local = query_width // head_dim
    pair_width = w_keyval.shape[1] * w_keyval.shape[2]
    key_width = pair_width // 2
    cache_local = prefix_keys.shape[1]
    cache_length = cache_local * seq_count
    first_row = seq_index * row_count
    hidden_f = hidden.astype(jnp.float32)
    normed = (
        hidden_f
        * lax.rsqrt(jnp.mean(hidden_f * hidden_f, axis=1, keepdims=True) + EPS)
        * gain.astype(jnp.float32)
    ).astype(jnp.bfloat16)
    segment, offset, prefix = row_tables(lengths, assignment, all_rows)
    positions = offset + cache_length
    own_positions = lax.dynamic_slice_in_dim(positions, first_row, row_count)
    own_segment = lax.dynamic_slice_in_dim(segment, first_row, row_count)
    own_prefix = lax.dynamic_slice_in_dim(prefix, first_row, row_count)

    w_pairs = w_keyval.reshape(w_keyval.shape[0], pair_width)
    block_width = math.gcd(query_width, pair_width)
    cache_width = 2 * head_dim
    assert 2 * cache_local == row_count and cache_width % block_width == 0
    cache_keys = jnp.concatenate([prefix_keys[0, :, 0, :], prefix_keys[1, :, 0, :]], axis=1)
    cache_values = jnp.concatenate([prefix_values[0, :, 0, :], prefix_values[1, :, 0, :]], axis=1)
    combined = jnp.concatenate(
        [w_query, w_pairs, jnp.concatenate([cache_keys, cache_values], axis=0)], axis=1
    )
    total_width = combined.shape[1]
    gathered = lax.all_gather(combined, "seq", axis=0, tiled=True)
    pairs_own = project(
        normed, gathered, kv_bias.reshape(pair_width).astype(jnp.float32),
        query_width // block_width, pair_width // block_width, block_width,
    )
    own_keys = rotate(
        pairs_own[:, :key_width].reshape(row_count, kv_local, head_dim), own_positions
    ).astype(jnp.bfloat16)
    own_values = (
        pairs_own[:, key_width:].reshape(row_count, kv_local, head_dim).astype(jnp.bfloat16)
    )
    pair_rows = jnp.concatenate(
        [own_keys.reshape(row_count, key_width), own_values.reshape(row_count, key_width)], axis=1
    )
    depth = 1
    near_rows = pair_rows
    while depth < 3:
        near_rows = jnp.concatenate([from_behind(near_rows, "seq", depth), near_rows], axis=0)
        depth = 2 * depth
    depth = depth - 1
    query_block = math.gcd(query_width, 4 * block_width)
    query_own = project(normed, gathered, q_bias.astype(jnp.float32), 0, query_width // query_block, query_block)
    own_queries = rotate(query_own.reshape(row_count, heads_local, head_dim), own_positions).astype(
        jnp.bfloat16
    )
    near_count = near_rows.shape[0]
    near_index = first_row - depth * row_count + jnp.arange(near_count, dtype=jnp.int32)
    near_segment = segment[jnp.clip(near_index, 0, all_rows - 1)]
    near_segment = jnp.where(near_index >= 0, near_segment, -1)
    col_info = jnp.concatenate(
        [near_segment[None, :], near_index[None, :], jnp.zeros((6, near_count), jnp.int32)], axis=0
    )
    own_rows = first_row + jnp.arange(row_count, dtype=jnp.int32)
    row_info = jnp.stack(
        [own_prefix, own_segment, own_rows, jnp.zeros_like(own_rows)], axis=1
    ).astype(jnp.int32)
    row_info = jnp.repeat(row_info, heads_local, axis=0)
    cache = gathered.reshape(seq_count, 2, cache_local, total_width)
    out_rows = attend(
        own_queries.reshape(row_count * heads_local, head_dim),
        row_info,
        col_info,
        cache,
        (query_width + pair_width) // head_dim,
        near_rows,
    )
    attention = out_rows.reshape(row_count, query_width)
    return (attention, own_keys, own_values)


def solution(mesh):
    in_specs = (
        P("seq", None),
        P(),
        P("seq", "tensor"),
        P("tensor"),
        P("seq", None, "tensor"),
        P(None, "tensor"),
        P(None, "seq", "tensor", None),
        P(None, "seq", "tensor", None),
        P(),
        P(),
    )
    out_specs = (P("seq", "tensor"), P("seq", "tensor", None), P("seq", "tensor", None))
    return jax.shard_map(local, mesh=mesh, in_specs=in_specs, out_specs=out_specs, check_vma=False)
```
